512 devices in a mesh: space: 16 (over z), chaos: 32 (over x, y, core).
Axes of the slice: x: 4, y: 4, z: 16, core: 2. Of those that a mesh axis runs over, the one named last changes fastest.
Arguments:
- forcing: float32 [960, 64, 128], P('chaos', 'space'), may hold values from -120 to 120
- mean_field: float32 [64, 128], P('space'), may hold values from 1 to 8
- modes: float32 [12, 64, 128], P(None, 'space'), may hold values from 0.02 to 0.05
- lengths: int32 [32], replicated, may hold values from 1 to 30, 455 in all
Outputs:
- solution: float32 [960, 64, 128], P('chaos', 'space')
- norms: float32 [3], replicated
The draws below stay inside these ranges and needn't reach their ends.
Inputs may be any that keep to these rules, and one draw needn't show every extreme that they name: Group lengths are positive, sum to 455, and the largest is exactly 30.
All inputs are finite; a program needn't handle non-finite values.
Results may differ from the reference program's by a relative error of at most 0.0001.
Values sent between devices are 32-bit elements; how exact they have to be, the bound alone decides.
No kernel may reach another device: no remote copies, remote signals or barrier semaphores. Data moves between devices by JAX's collectives and lax.ppermute only.
A program may use at most 64 MiB of HBM per device.

```python
import math
import jax
import jax.numpy as jnp
import numpy as np
from jax import lax

M = 12
P_SIZE = 455
CAP = 30
SLOTS = 960
COLS = 128
NX = 64
ITERS = 3
N_CHAOS = 32


def draw_forcing(key, part):
    first_key, second_key, third_key = jax.random.split(key, 3)
    slot_place = jnp.arange(SLOTS, dtype=jnp.float32) / SLOTS
    row_place = jnp.arange(NX, dtype=jnp.float32) / NX
    slot_scale = jnp.exp(jax.random.uniform(second_key, (SLOTS,), jnp.float32) * math.log(10.0)) * (1.0 + 0.7 * slot_place)
    row_scale = 1.0 + 0.7 * row_place
    common = jnp.clip(jax.random.normal(third_key, (NX, COLS), jnp.float32), -2.9, 2.9)
    single = jnp.clip(jax.random.normal(first_key, (SLOTS, NX, COLS), jnp.float32), -2.9, 2.9)
    base = 0.7 * (common[None, :, :] + single)
    return base * slot_scale[:, None, None] * row_scale[None, :, None]


def levels(rng, shape, pieces, smallest, high):
    level, own = 1.0, jax.random.fold_in(rng, 6)
    for axis_at, parts in pieces:
        heights = jnp.exp(jax.random.uniform(jax.random.fold_in(own, axis_at), (parts,), jnp.float32, smallest / len(pieces), high / len(pieces)))
        level = level * jnp.repeat(heights, shape[axis_at] // parts).reshape([-1 if axis == axis_at else 1 for axis in range(len(shape))])
    return level


def profile(number_of, total, reach, lean):
    loads = [(1 << 20) // math.isqrt(grade ** lean) + 1 for grade in range(2, number_of + 1)]
    spare, holding = total - reach - (number_of - 1), [1] * (number_of - 1)
    while spare > 0:
        candidates = [i for i in range(number_of - 1) if holding[i] < reach]
        pool, budget = sum([loads[i] for i in candidates]), spare
        for i in candidates:
            extra = min(reach - holding[i], max(1, budget * loads[i] // pool), spare)
            holding[i] = holding[i] + extra
            spare = spare - extra
    return np.array([reach] + holding)


def uneven(own_key, amount, total, most, skew):
    if amount == 2:
        one = jax.random.randint(own_key, (), max(1, total - most), min(most, total - 1) + 1)
        return jnp.stack([one, total - one])
    sizes = jnp.asarray(profile(amount, total, most, skew), jnp.int32)
    twos = (amount - 1) // 2
    donor, sink = sizes[1:1 + 2 * twos:2], sizes[2:2 + 2 * twos:2]
    slack = jnp.minimum(donor - 1, most - sink)
    moved = jax.random.randint(jax.random.fold_in(own_key, 1), (twos,), 0, 1 << 20) % (slack + 1)
    sizes = sizes.at[1:1 + 2 * twos:2].set(donor - moved).at[2:2 + 2 * twos:2].set(sink + moved)
    return sizes[jax.random.permutation(jax.random.fold_in(own_key, 2), amount)]


def setup_inputs(seed: int = 0) -> dict:
    streams_of = jax.random.split(jax.random.key(seed), 5)
    forcing = draw_forcing(jax.random.fold_in(streams_of[4], 71), 0)
    mean_field = jnp.clip(jnp.exp(math.log(8.0) - 2.0794415 * jax.random.uniform(streams_of[1], (NX, COLS), jnp.float32) ** levels(streams_of[1], (NX, COLS), ((0, 16),), -0.2, 0.2)), 1.0, 8.0)
    modes = jnp.clip(0.02 + 0.030000001 * jax.random.uniform(streams_of[2], (M, NX, COLS), jnp.float32) ** levels(streams_of[2], (M, NX, COLS), ((1, 16),), -0.2, 0.2), 0.02, 0.05)
    lengths = uneven(streams_of[3], N_CHAOS, P_SIZE, CAP, 2).astype(jnp.int32)
    return {"forcing": forcing, "mean_field": mean_field, "modes": modes, "lengths": lengths}


spectrum_low = 0.05
spectrum_high = 3.0

def index_key(entry):
    return tuple((int(value) for value in entry))

def chaos_tables(terms):
    indices = [np.zeros(terms, dtype=np.int64)]
    for first in range(terms):
        entry = np.zeros(terms, dtype=np.int64)
        entry[first] += 1
        indices.append(entry)
    for first in range(terms):
        for second in range(first, terms):
            entry = np.zeros(terms, dtype=np.int64)
            entry[first] += 1
            entry[second] += 1
            indices.append(entry)
    for first in range(terms):
        for second in range(first, terms):
            for third in range(second, terms):
                entry = np.zeros(terms, dtype=np.int64)
                entry[first] += 1
                entry[second] += 1
                entry[third] += 1
                indices.append(entry)
    lookup = {}
    for number, entry in enumerate(indices):
        lookup[index_key(entry)] = number
    count = len(indices)
    upward = np.full((count, terms), count, dtype=np.int64)
    downward = np.full((count, terms), count, dtype=np.int64)
    up_coef = np.zeros((count, terms))
    down_coef = np.zeros((count, terms))
    for number, entry in enumerate(indices):
        for term in range(terms):
            if entry.sum() < 3:
                other = entry.copy()
                other[term] += 1
                upward[number, term] = lookup[index_key(other)]
                up_coef[number, term] = math.sqrt(entry[term] + 1)
            if entry[term] > 0:
                other = entry.copy()
                other[term] -= 1
                downward[number, term] = lookup[index_key(other)]
                down_coef[number, term] = math.sqrt(entry[term])
    return (upward.astype(np.int32), downward.astype(np.int32), up_coef.astype(np.float32), down_coef.astype(np.float32))

def shifted(values, toward):
    blank = jnp.zeros_like(values[..., :1])
    if toward > 0:
        return jnp.concatenate([values[..., 1:], blank], axis=-1)
    return jnp.concatenate([blank, values[..., :-1]], axis=-1)

def stiffness(field_pad, tile_pad):
    center_field = field_pad[..., 1:-1, :]
    center_tile = tile_pad[..., 1:-1, :]
    result = 0.5 * (center_field + field_pad[..., :-2, :]) * (center_tile - tile_pad[..., :-2, :])
    result = result + 0.5 * (center_field + field_pad[..., 2:, :]) * (center_tile - tile_pad[..., 2:, :])
    for toward in (1, -1):
        result = result + 0.5 * (center_field + shifted(center_field, toward)) * (center_tile - shifted(center_tile, toward))
    return result

def diagonal_of(field_pad):
    center_field = field_pad[..., 1:-1, :]
    result = 0.5 * (center_field + field_pad[..., :-2, :])
    result = result + 0.5 * (center_field + field_pad[..., 2:, :])
    for toward in (1, -1):
        result = result + 0.5 * (center_field + shifted(center_field, toward))
    return result

def pad_rows(values):
    widths = [(0, 0)] * (values.ndim - 2) + [(1, 1), (0, 0)]
    return jnp.pad(values, widths)

def reference(forcing, mean_field, modes, lengths):
    upward, downward, up_coef, down_coef = chaos_tables(M)
    up_table = jnp.asarray(upward, dtype=jnp.int32)
    down_table = jnp.asarray(downward, dtype=jnp.int32)
    up_values = jnp.asarray(up_coef, dtype=jnp.float32)
    down_values = jnp.asarray(down_coef, dtype=jnp.float32)
    slot_cap = forcing.shape[0] // N_CHAOS
    group_ends = jnp.cumsum(lengths).astype(jnp.int32)
    group_starts = (group_ends - lengths).astype(jnp.int32)
    coeff_index = jnp.arange(P_SIZE, dtype=jnp.int32)
    owner = lax.optimization_barrier(jnp.sum((coeff_index[:, None] >= group_ends[None, :]).astype(jnp.int32), axis=1)).astype(jnp.int32)
    slot_of = (owner * slot_cap + coeff_index - group_starts[owner]).astype(jnp.int32)
    rhs = forcing[slot_of]
    field_pad = pad_rows(mean_field)
    diagonal = diagonal_of(field_pad)

    def operator(tiles):
        extended = jnp.concatenate([tiles, jnp.zeros((1,) + tiles.shape[1:], jnp.float32)], axis=0)
        total = stiffness(field_pad, pad_rows(tiles))

        def one_term(carry, inputs):
            up_index, down_index, up_weight, down_weight, mode = inputs
            coupled = up_weight[:, None, None] * extended[up_index] + down_weight[:, None, None] * extended[down_index]
            return (carry + stiffness(pad_rows(mean_field * mode), pad_rows(coupled)), None)
        total, unused = lax.scan(one_term, total, (up_table.T, down_table.T, up_values.T, down_values.T, modes))
        return total
    theta = (spectrum_high + spectrum_low) / 2.0
    delta = (spectrum_high - spectrum_low) / 2.0
    sigma = theta / delta
    rho = 1.0 / sigma
    residual = rhs
    solution = jnp.zeros_like(rhs)
    direction = residual / diagonal / theta
    norm_list = []
    for sweep_index in range(ITERS):
        solution = solution + direction
        residual = residual - operator(direction)
        norm_list.append(jnp.sqrt(jnp.sum(residual * residual)))
        if sweep_index + 1 < ITERS:
            rho_new = 1.0 / (2.0 * sigma - rho)
            direction = rho_new * rho * direction + 2.0 * rho_new / delta * (residual / diagonal)
            rho = rho_new
    output = jnp.zeros_like(forcing).at[slot_of].set(solution)
    return (output, jnp.stack(norm_list))
```

```python
import math

import jax
import jax.numpy as jnp
import numpy as np
from jax import lax
from jax.sharding import PartitionSpec as P

M = 12
P_SIZE = 455
ITERS = 3
GHOST = ITERS + 1


spectrum_low = 0.05
spectrum_high = 3.0


def index_key(entry):
    return tuple((int(value) for value in entry))


def chaos_tables(terms):
    indices = [np.zeros(terms, dtype=np.int64)]
    for first in range(terms):
        entry = np.zeros(terms, dtype=np.int64)
        entry[first] += 1
        indices.append(entry)
    for first in range(terms):
        for second in range(first, terms):
            entry = np.zeros(terms, dtype=np.int64)
            entry[first] += 1
            entry[second] += 1
            indices.append(entry)
    for first in range(terms):
        for second in range(first, terms):
            for third in range(second, terms):
                entry = np.zeros(terms, dtype=np.int64)
                entry[first] += 1
                entry[second] += 1
                entry[third] += 1
                indices.append(entry)
    lookup = {}
    for number, entry in enumerate(indices):
        lookup[index_key(entry)] = number
    count = len(indices)
    upward = np.full((count, terms), count, dtype=np.int64)
    downward = np.full((count, terms), count, dtype=np.int64)
    up_coef = np.zeros((count, terms))
    down_coef = np.zeros((count, terms))
    for number, entry in enumerate(indices):
        for term in range(terms):
            if entry.sum() < 3:
                other = entry.copy()
                other[term] += 1
                upward[number, term] = lookup[index_key(other)]
                up_coef[number, term] = math.sqrt(entry[term] + 1)
            if entry[term] > 0:
                other = entry.copy()
                other[term] -= 1
                downward[number, term] = lookup[index_key(other)]
                down_coef[number, term] = math.sqrt(entry[term])
    return (
        upward.astype(np.int32),
        downward.astype(np.int32),
        up_coef.astype(np.float32),
        down_coef.astype(np.float32),
    )


def neighbour(values, step):
    blank = jnp.zeros(values.shape[:-1] + (abs(step),), values.dtype)
    if step > 0:
        return jnp.concatenate([values[..., step:], blank], axis=-1)
    return jnp.concatenate([blank, values[..., :step]], axis=-1)


def local(forcing, mean_field, modes, lengths):
    cap, rows, cols = forcing.shape
    n_space = lax.axis_size("space")
    n_chaos = lax.axis_size("chaos")
    my_row_block = lax.axis_index("space")
    my_col_block = lax.axis_index("chaos")
    width = cols // n_chaos
    ghost = GHOST
    assert rows >= ghost and ghost % width == 0 and width * n_chaos == cols
    patch_rows, patch_cols = rows + 2 * ghost, width + 2 * ghost
    cells = patch_rows * patch_cols
    count = P_SIZE

    fields = jnp.concatenate([mean_field[None], mean_field[None] * modes], axis=0)
    block = jnp.concatenate([forcing, fields], axis=0)
    down_pairs = [(i, i + 1) for i in range(n_space - 1)]
    up_pairs = [(i + 1, i) for i in range(n_space - 1)]
    above = lax.ppermute(block[:, rows - ghost :], "space", down_pairs)
    below = lax.ppermute(block[:, :ghost], "space", up_pairs)
    tall = jnp.concatenate([above, block, below], axis=1)
    tall = jnp.pad(tall, ((0, 0), (0, 0), (ghost, ghost)))

    side = ghost // width
    pieces = tall.reshape(tall.shape[0], patch_rows, n_chaos + 2 * side, width)
    windows = jnp.concatenate(
        [pieces[:, :, j : j + n_chaos] for j in range(2 * side + 1)], axis=-1
    )
    sent = jnp.transpose(windows[:cap], (2, 0, 1, 3))
    got = lax.all_to_all(sent, "chaos", 0, 0, tiled=True)
    by_slot = got.reshape(n_chaos * cap, cells)
    my_fields = lax.dynamic_index_in_dim(windows[cap:], my_col_block, axis=2, keepdims=False)
    my_fields = my_fields.reshape(M + 1, cells)

    group_ends = jnp.cumsum(lengths).astype(jnp.int32)
    group_starts = (group_ends - lengths).astype(jnp.int32)
    coeff_index = jnp.arange(count, dtype=jnp.int32)
    owner = jnp.sum((coeff_index[:, None] >= group_ends[None, :]).astype(jnp.int32), axis=1)
    slot_of = (owner * cap + coeff_index - group_starts[owner]).astype(jnp.int32)
    rhs = jnp.take(by_slot, slot_of, axis=0)

    row_at = my_row_block * rows - ghost + jnp.arange(patch_rows)
    col_at = my_col_block * width - ghost + jnp.arange(patch_cols)
    inside = ((row_at >= 0) & (row_at < rows * n_space))[:, None] & (
        (col_at >= 0) & (col_at < cols)
    )[None, :]
    inside = inside.reshape(cells)
    local_rows = jnp.arange(patch_rows)
    local_cols = jnp.arange(patch_cols)
    own = ((local_rows >= ghost) & (local_rows < ghost + rows))[:, None] & (
        (local_cols >= ghost) & (local_cols < ghost + width)
    )[None, :]
    own = own.reshape(cells)

    steps = (-patch_cols, patch_cols, 1, -1)
    weights = jnp.stack([0.5 * (my_fields + neighbour(my_fields, s)) for s in steps], axis=1)
    mean_now = my_fields[0]
    diagonal = 0.5 * (mean_now + neighbour(mean_now, steps[0]))
    for s in steps[1:]:
        diagonal = diagonal + 0.5 * (mean_now + neighbour(mean_now, s))

    upward, downward, up_coef, down_coef = chaos_tables(M)
    rows_per_term = count + 1
    up_flat = (upward.T + rows_per_term * np.arange(M)[:, None]).reshape(-1)
    down_flat = (downward.T + rows_per_term * np.arange(M)[:, None]).reshape(-1)
    up_w = jnp.asarray(up_coef.T[:, :, None])
    down_w = jnp.asarray(down_coef.T[:, :, None])

    def operator(tiles):
        diffs = [tiles - neighbour(tiles, s) for s in steps]
        terms = weights[:, 0][:, None] * diffs[0][None]
        for n in range(1, 4):
            terms = terms + weights[:, n][:, None] * diffs[n][None]
        coupled = jnp.concatenate(
            [terms[1:], jnp.zeros((M, 1, cells), jnp.float32)], axis=1
        ).reshape(M * rows_per_term, cells)
        up_part = jnp.take(coupled, up_flat, axis=0).reshape(M, count, cells)
        down_part = jnp.take(coupled, down_flat, axis=0).reshape(M, count, cells)
        return terms[0] + jnp.sum(up_w * up_part + down_w * down_part, axis=0)

    theta = (spectrum_high + spectrum_low) / 2.0
    delta = (spectrum_high - spectrum_low) / 2.0
    sigma = theta / delta
    rho = 1.0 / sigma
    residual = rhs
    solution = jnp.zeros_like(rhs)
    direction = jnp.where(inside, residual / diagonal / theta, 0.0)
    partial_list = []
    for sweep_index in range(ITERS):
        solution = solution + direction
        residual = residual - operator(direction)
        partial_list.append(jnp.sum(jnp.where(own, residual * residual, 0.0)))
        if sweep_index + 1 < ITERS:
            rho_new = 1.0 / (2.0 * sigma - rho)
            direction = rho_new * rho * direction + 2.0 * rho_new / delta * (residual / diagonal)
            direction = jnp.where(inside, direction, 0.0)
            rho = rho_new
    partials = jnp.stack(partial_list)

    mine = solution.reshape(count, patch_rows, patch_cols)[
        :, ghost : ghost + rows, ghost : ghost + width
    ]
    mine = jnp.concatenate([mine, jnp.zeros((1, rows, width), jnp.float32)], axis=0)
    slot_index = jnp.arange(cap, dtype=jnp.int32)
    live = slot_index[None, :] < lengths[:, None]
    coeff_of_slot = jnp.where(live, group_starts[:, None] + slot_index[None, :], count)
    by_slot_out = jnp.take(mine, coeff_of_slot.reshape(-1), axis=0)
    chunk = cap * rows * width
    payload = jnp.concatenate(
        [
            by_slot_out.reshape(n_chaos, chunk),
            jnp.broadcast_to(partials[None, :], (n_chaos, ITERS)),
        ],
        axis=1,
    )
    back = lax.all_to_all(payload, "chaos", 0, 0, tiled=True)
    out = back[:, :chunk].reshape(n_chaos, cap, rows, width)
    out = jnp.transpose(out, (1, 2, 0, 3)).reshape(cap, rows, cols)
    row_sum = jnp.sum(back[:, chunk:], axis=0)
    norms = jnp.sqrt(lax.psum(row_sum, "space"))
    return (out, norms)


def solution(mesh):
    in_specs = (P("chaos", "space", None), P("space", None), P(None, "space", None), P())
    out_specs = (P("chaos", "space", None), P())
    return jax.shard_map(local, mesh=mesh, in_specs=in_specs, out_specs=out_specs, check_vma=False)
```

```python
import math

import jax
import jax.numpy as jnp
import numpy as np
from jax import lax
from jax.sharding import PartitionSpec as P

M = 12
P_SIZE = 455
ITERS = 3
GHOST = ITERS + 1


spectrum_low = 0.05
spectrum_high = 3.0


def index_key(entry):
    return tuple((int(value) for value in entry))


def chaos_tables(terms):
    indices = [np.zeros(terms, dtype=np.int64)]
    for first in range(terms):
        entry = np.zeros(terms, dtype=np.int64)
        entry[first] += 1
        indices.append(entry)
    for first in range(terms):
        for second in range(first, terms):
            entry = np.zeros(terms, dtype=np.int64)
            entry[first] += 1
            entry[second] += 1
            indices.append(entry)
    for first in range(terms):
        for second in range(first, terms):
            for third in range(second, terms):
                entry = np.zeros(terms, dtype=np.int64)
                entry[first] += 1
                entry[second] += 1
                entry[third] += 1
                indices.append(entry)
    lookup = {}
    for number, entry in enumerate(indices):
        lookup[index_key(entry)] = number
    count = len(indices)
    upward = np.full((count, terms), count, dtype=np.int64)
    downward = np.full((count, terms), count, dtype=np.int64)
    up_coef = np.zeros((count, terms))
    down_coef = np.zeros((count, terms))
    for number, entry in enumerate(indices):
        for term in range(terms):
            if entry.sum() < 3:
                other = entry.copy()
                other[term] += 1
                upward[number, term] = lookup[index_key(other)]
                up_coef[number, term] = math.sqrt(entry[term] + 1)
            if entry[term] > 0:
                other = entry.copy()
                other[term] -= 1
                downward[number, term] = lookup[index_key(other)]
                down_coef[number, term] = math.sqrt(entry[term])
    return (
        upward.astype(np.int32),
        downward.astype(np.int32),
        up_coef.astype(np.float32),
        down_coef.astype(np.float32),
    )


def degree_layout(terms):
    sizes = [1, terms, terms * (terms + 1) // 2, terms * (terms + 1) * (terms + 2) // 6]
    firsts = np.cumsum([0] + sizes[:-1])
    padded = [-(-size // 8) * 8 for size in sizes]
    offsets = np.cumsum([0] + padded[:-1])
    return sizes, firsts, padded, offsets


def coupling_blocks(terms):
    upward, downward, up_coef, down_coef = chaos_tables(terms)
    sizes, firsts, padded, offsets = degree_layout(terms)
    count = sum(sizes)
    total = sum(padded)
    row_of = np.zeros(count, np.int64)
    for d in range(4):
        row_of[firsts[d] : firsts[d] + sizes[d]] = offsets[d] + np.arange(sizes[d])
    dense = np.zeros((terms, total, total), np.float64)
    for p in range(count):
        for k in range(terms):
            if upward[p, k] < count:
                dense[k, row_of[p], row_of[upward[p, k]]] = up_coef[p, k]
            if downward[p, k] < count:
                dense[k, row_of[p], row_of[downward[p, k]]] = down_coef[p, k]

    def block(out_degrees, in_degree):
        rows = np.concatenate([offsets[d] + np.arange(padded[d]) for d in out_degrees])
        cols = offsets[in_degree] + np.arange(padded[in_degree])
        part = dense[:, rows][:, :, cols]
        return np.transpose(part, (1, 0, 2)).reshape(len(rows), terms * len(cols)).astype(np.float32)

    return {
        0: block((1,), 0),
        1: block((0, 2), 1),
        2: block((1, 3), 2),
        3: block((2,), 3),
    }, row_of, total


def neighbour(values, step):
    blank = jnp.zeros(values.shape[:-1] + (abs(step),), values.dtype)
    if step > 0:
        return jnp.concatenate([values[..., step:], blank], axis=-1)
    return jnp.concatenate([blank, values[..., :step]], axis=-1)


def local(forcing, mean_field, modes, lengths):
    cap, rows, cols = forcing.shape
    n_space = lax.axis_size("space")
    n_chaos = lax.axis_size("chaos")
    my_row_block = lax.axis_index("space")
    my_col_block = lax.axis_index("chaos")
    width = cols // n_chaos
    ghost = GHOST
    assert rows >= ghost and ghost % width == 0 and width * n_chaos == cols
    patch_rows, patch_cols = rows + 2 * ghost, width + 2 * ghost
    cells = patch_rows * patch_cols
    count = P_SIZE

    fields = jnp.concatenate([mean_field[None], mean_field[None] * modes], axis=0)
    block = jnp.concatenate([forcing, fields], axis=0)
    down_pairs = [(i, i + 1) for i in range(n_space - 1)]
    up_pairs = [(i + 1, i) for i in range(n_space - 1)]
    above = lax.ppermute(block[:, rows - ghost :], "space", down_pairs)
    below = lax.ppermute(block[:, :ghost], "space", up_pairs)
    tall = jnp.concatenate([above, block, below], axis=1)
    tall = jnp.pad(tall, ((0, 0), (0, 0), (ghost, ghost)))

    side = ghost // width
    pieces = tall.reshape(tall.shape[0], patch_rows, n_chaos + 2 * side, width)
    windows = jnp.concatenate(
        [pieces[:, :, j : j + n_chaos] for j in range(2 * side + 1)], axis=-1
    )
    sent = jnp.transpose(windows[:cap], (2, 0, 1, 3))
    got = lax.all_to_all(sent, "chaos", 0, 0, tiled=True)
    by_slot = got.reshape(n_chaos * cap, cells)
    my_fields = lax.dynamic_index_in_dim(windows[cap:], my_col_block, axis=2, keepdims=False)
    my_fields = my_fields.reshape(M + 1, cells)

    blocks, row_of, total = coupling_blocks(M)
    sizes, firsts, padded, offsets = degree_layout(M)
    coeff_of_row = np.full(total, -1, np.int64)
    coeff_of_row[row_of] = np.arange(count)
    row_coeff = jnp.asarray(np.maximum(coeff_of_row, 0), jnp.int32)
    group_ends = jnp.cumsum(lengths).astype(jnp.int32)
    group_starts = (group_ends - lengths).astype(jnp.int32)
    skipped = jnp.sum(
        jnp.where(row_coeff[:, None] >= group_ends[None, :], cap - lengths[None, :], 0), axis=1
    )
    slot_of_row = jnp.where(jnp.asarray(coeff_of_row >= 0), row_coeff + skipped, n_chaos * cap)
    by_slot = jnp.concatenate([by_slot, jnp.zeros((1, cells), jnp.float32)], axis=0)
    rhs = jnp.take(by_slot, slot_of_row, axis=0)

    row_at = my_row_block * rows - ghost + jnp.arange(patch_rows)
    col_at = my_col_block * width - ghost + jnp.arange(patch_cols)
    inside = ((row_at >= 0) & (row_at < rows * n_space))[:, None] & (
        (col_at >= 0) & (col_at < cols)
    )[None, :]
    inside = inside.reshape(cells)
    local_rows = jnp.arange(patch_rows)
    local_cols = jnp.arange(patch_cols)
    own = ((local_rows >= ghost) & (local_rows < ghost + rows))[:, None] & (
        (local_cols >= ghost) & (local_cols < ghost + width)
    )[None, :]
    own = own.reshape(cells)

    steps = (-patch_cols, patch_cols, 1, -1)
    weights = jnp.stack([0.5 * (my_fields + neighbour(my_fields, s)) for s in steps], axis=1)
    mean_now = my_fields[0]
    diagonal = 0.5 * (mean_now + neighbour(mean_now, steps[0]))
    for s in steps[1:]:
        diagonal = diagonal + 0.5 * (mean_now + neighbour(mean_now, s))

    mats = {d: jnp.asarray(blocks[d]) for d in blocks}

    def mix(matrix, stacked):
        return jnp.dot(
            matrix, stacked, precision=lax.Precision.HIGHEST, preferred_element_type=jnp.float32
        )

    def operator(tiles):
        diffs = [tiles - neighbour(tiles, s) for s in steps]
        terms = weights[:, 0][:, None] * diffs[0][None]
        for n in range(1, 4):
            terms = terms + weights[:, n][:, None] * diffs[n][None]

        def stacked(d):
            return terms[1:, offsets[d] : offsets[d] + padded[d]].reshape(M * padded[d], cells)

        from0 = mix(mats[0], stacked(0))
        from1 = mix(mats[1], stacked(1))
        from2 = mix(mats[2], stacked(2))
        from3 = mix(mats[3], stacked(3))
        p0, p1 = padded[0], padded[1]
        coupled = jnp.concatenate(
            [from1[:p0], from2[:p1] + from0, from3 + from1[p0:], from2[p1:]], axis=0
        )
        return terms[0] + coupled

    theta = (spectrum_high + spectrum_low) / 2.0
    delta = (spectrum_high - spectrum_low) / 2.0
    sigma = theta / delta
    rho = 1.0 / sigma
    residual = rhs
    solution = jnp.zeros_like(rhs)
    direction = jnp.where(inside, residual / diagonal / theta, 0.0)
    partial_list = []
    for sweep_index in range(ITERS):
        solution = solution + direction
        residual = residual - operator(direction)
        partial_list.append(jnp.sum(jnp.where(own, residual * residual, 0.0)))
        if sweep_index + 1 < ITERS:
            rho_new = 1.0 / (2.0 * sigma - rho)
            direction = rho_new * rho * direction + 2.0 * rho_new / delta * (residual / diagonal)
            direction = jnp.where(inside, direction, 0.0)
            rho = rho_new
    partials = jnp.stack(partial_list)

    mine = solution.reshape(total, patch_rows, patch_cols)[
        :, ghost : ghost + rows, ghost : ghost + width
    ]
    mine = jnp.concatenate([mine, jnp.zeros((1, rows, width), jnp.float32)], axis=0)
    slot_index = jnp.arange(cap, dtype=jnp.int32)
    live = slot_index[None, :] < lengths[:, None]
    coeff = group_starts[:, None] + slot_index[None, :]
    shift = jnp.zeros_like(coeff)
    for d in range(1, 4):
        shift = jnp.where(coeff >= firsts[d], int(offsets[d] - firsts[d]), shift)
    row_of_slot = jnp.where(live, coeff + shift, total)
    by_slot_out = jnp.take(mine, row_of_slot.reshape(-1), axis=0)
    chunk = cap * rows * width
    payload = jnp.concatenate(
        [
            by_slot_out.reshape(n_chaos, chunk),
            jnp.broadcast_to(partials[None, :], (n_chaos, ITERS)),
        ],
        axis=1,
    )
    back = lax.all_to_all(payload, "chaos", 0, 0, tiled=True)
    out = back[:, :chunk].reshape(n_chaos, cap, rows, width)
    out = jnp.transpose(out, (1, 2, 0, 3)).reshape(cap, rows, cols)
    row_sum = jnp.sum(back[:, chunk:], axis=0)
    spread = jnp.broadcast_to(row_sum[None, :], (n_space, ITERS))
    all_rows = lax.all_to_all(spread, "space", 0, 0, tiled=True)
    norms = jnp.sqrt(jnp.sum(all_rows, axis=0))
    return (out, norms)


def solution(mesh):
    in_specs = (P("chaos", "space", None), P("space", None), P(None, "space", None), P())
    out_specs = (P("chaos", "space", None), P())
    return jax.shard_map(local, mesh=mesh, in_specs=in_specs, out_specs=out_specs, check_vma=False)
```

```python
import functools
import math

import jax
import jax.numpy as jnp
import numpy as np
from jax import lax
from jax.experimental import pallas as pl
from jax.experimental.pallas import tpu as pltpu
from jax.sharding import PartitionSpec as P

M = 12
P_SIZE = 455
ITERS = 3
GHOST = ITERS + 1


spectrum_low = 0.05
spectrum_high = 3.0


def index_key(entry):
    return tuple((int(value) for value in entry))


def chaos_tables(terms):
    indices = [np.zeros(terms, dtype=np.int64)]
    for first in range(terms):
        entry = np.zeros(terms, dtype=np.int64)
        entry[first] += 1
        indices.append(entry)
    for first in range(terms):
        for second in range(first, terms):
            entry = np.zeros(terms, dtype=np.int64)
            entry[first] += 1
            entry[second] += 1
            indices.append(entry)
    for first in range(terms):
        for second in range(first, terms):
            for third in range(second, terms):
                entry = np.zeros(terms, dtype=np.int64)
                entry[first] += 1
                entry[second] += 1
                entry[third] += 1
                indices.append(entry)
    lookup = {}
    for number, entry in enumerate(indices):
        lookup[index_key(entry)] = number
    count = len(indices)
    upward = np.full((count, terms), count, dtype=np.int64)
    downward = np.full((count, terms), count, dtype=np.int64)
    up_coef = np.zeros((count, terms))
    down_coef = np.zeros((count, terms))
    for number, entry in enumerate(indices):
        for term in range(terms):
            if entry.sum() < 3:
                other = entry.copy()
                other[term] += 1
                upward[number, term] = lookup[index_key(other)]
                up_coef[number, term] = math.sqrt(entry[term] + 1)
            if entry[term] > 0:
                other = entry.copy()
                other[term] -= 1
                downward[number, term] = lookup[index_key(other)]
                down_coef[number, term] = math.sqrt(entry[term])
    return (
        upward.astype(np.int32),
        downward.astype(np.int32),
        up_coef.astype(np.float32),
        down_coef.astype(np.float32),
    )


def degree_layout(terms):
    sizes = [1, terms, terms * (terms + 1) // 2, terms * (terms + 1) * (terms + 2) // 6]
    firsts = np.cumsum([0] + sizes[:-1])
    padded = [-(-size // 8) * 8 for size in sizes]
    offsets = np.cumsum([0] + padded[:-1])
    return sizes, firsts, padded, offsets


def coupling_blocks(terms):
    upward, downward, up_coef, down_coef = chaos_tables(terms)
    sizes, firsts, padded, offsets = degree_layout(terms)
    count = sum(sizes)
    total = sum(padded)
    row_of = np.zeros(count, np.int64)
    for d in range(4):
        row_of[firsts[d] : firsts[d] + sizes[d]] = offsets[d] + np.arange(sizes[d])
    dense = np.zeros((terms, total, total), np.float64)
    for p in range(count):
        for k in range(terms):
            if upward[p, k] < count:
                dense[k, row_of[p], row_of[upward[p, k]]] = up_coef[p, k]
            if downward[p, k] < count:
                dense[k, row_of[p], row_of[downward[p, k]]] = down_coef[p, k]

    def block(out_degrees, in_degree):
        rows = np.concatenate([offsets[d] + np.arange(padded[d]) for d in out_degrees])
        cols = offsets[in_degree] + np.arange(padded[in_degree])
        part = dense[:, rows][:, :, cols]
        return np.transpose(part, (1, 0, 2)).reshape(len(rows), terms * len(cols)).astype(np.float32)

    return {
        0: block((1,), 0),
        1: block((0, 2), 1),
        2: block((1, 3), 2),
        3: block((2,), 3),
    }, row_of, total


def neighbour(values, step):
    blank = jnp.zeros(values.shape[:-1] + (abs(step),), values.dtype)
    if step > 0:
        return jnp.concatenate([values[..., step:], blank], axis=-1)
    return jnp.concatenate([blank, values[..., :step]], axis=-1)


def sweeps(rhs_ref, field_ref, mask_ref, w0_ref, w1_ref, w2_ref, w3_ref, sol_ref, part_ref,
           s0_ref, s1_ref, s2_ref, s3_ref, *, padded, offsets, cols):
    lanes = rhs_ref.shape[1]
    shifts = (cols, lanes - cols, lanes - 1, 1)

    def near(values, shift):
        return pltpu.roll(values, shift, 1)

    fields = field_ref[...]
    inside = mask_ref[0:1, :] > 0.5
    own = mask_ref[1:2, :] > 0.5
    weights = [[0.5 * (fields[k : k + 1] + near(fields, s)[k : k + 1]) for s in shifts] for k in range(M + 1)]
    mean_now = fields[0:1]
    diagonal = 0.5 * (mean_now + near(mean_now, shifts[0]))
    for s in shifts[1:]:
        diagonal = diagonal + 0.5 * (mean_now + near(mean_now, s))
    diagonal = jnp.where(inside, diagonal, 1.0)
    stacks = (s0_ref, s1_ref, s2_ref, s3_ref)
    mats = (w0_ref, w1_ref, w2_ref, w3_ref)

    def operator(tiles):
        diffs = [tiles - near(tiles, s) for s in shifts]
        base = None
        for k in range(M + 1):
            term = weights[k][0] * diffs[0]
            for n in range(1, 4):
                term = term + weights[k][n] * diffs[n]
            if k == 0:
                base = term
                continue
            for d in range(4):
                stacks[d][(k - 1) * padded[d] : k * padded[d], :] = term[offsets[d] : offsets[d] + padded[d]]
        mixed = [
            jnp.dot(mats[d][...], stacks[d][...], precision=lax.Precision.HIGHEST, preferred_element_type=jnp.float32)
            for d in range(4)
        ]
        p0, p1 = padded[0], padded[1]
        coupled = jnp.concatenate(
            [mixed[1][:p0], mixed[2][:p1] + mixed[0], mixed[3] + mixed[1][p0:], mixed[2][p1:]], axis=0
        )
        return base + coupled

    theta = (spectrum_high + spectrum_low) / 2.0
    delta = (spectrum_high - spectrum_low) / 2.0
    sigma = theta / delta
    rho = 1.0 / sigma
    residual = rhs_ref[...]
    solution = jnp.zeros_like(residual)
    direction = jnp.where(inside, residual / diagonal / theta, 0.0)
    lane = lax.broadcasted_iota(jnp.int32, (8, 128), 1)
    partial_out = jnp.zeros((8, 128), jnp.float32)
    for sweep_index in range(ITERS):
        solution = solution + direction
        residual = residual - operator(direction)
        value = jnp.sum(jnp.where(own, residual * residual, 0.0))
        partial_out = jnp.where(lane == sweep_index, value, partial_out)
        if sweep_index + 1 < ITERS:
            rho_new = 1.0 / (2.0 * sigma - rho)
            direction = rho_new * rho * direction + 2.0 * rho_new / delta * (residual / diagonal)
            direction = jnp.where(inside, direction, 0.0)
            rho = rho_new
    sol_ref[...] = solution
    part_ref[...] = partial_out


def local(forcing, mean_field, modes, lengths):
    cap, rows, cols = forcing.shape
    n_space = lax.axis_size("space")
    n_chaos = lax.axis_size("chaos")
    my_row_block = lax.axis_index("space")
    my_col_block = lax.axis_index("chaos")
    width = cols // n_chaos
    ghost = GHOST
    assert rows >= ghost and ghost % width == 0 and width * n_chaos == cols
    patch_rows, patch_cols = rows + 2 * ghost, width + 2 * ghost
    cells = patch_rows * patch_cols
    count = P_SIZE

    fields = jnp.concatenate([mean_field[None], mean_field[None] * modes], axis=0)
    block = jnp.concatenate([forcing, fields], axis=0)
    down_pairs = [(i, i + 1) for i in range(n_space - 1)]
    up_pairs = [(i + 1, i) for i in range(n_space - 1)]
    above = lax.ppermute(block[:, rows - ghost :], "space", down_pairs)
    below = lax.ppermute(block[:, :ghost], "space", up_pairs)
    tall = jnp.concatenate([above, block, below], axis=1)
    tall = jnp.pad(tall, ((0, 0), (0, 0), (ghost, ghost)))

    side = ghost // width
    pieces = tall.reshape(tall.shape[0], patch_rows, n_chaos + 2 * side, width)
    windows = jnp.concatenate(
        [pieces[:, :, j : j + n_chaos] for j in range(2 * side + 1)], axis=-1
    )
    sent = jnp.transpose(windows[:cap], (2, 0, 1, 3))
    got = lax.all_to_all(sent, "chaos", 0, 0, tiled=True)
    by_slot = got.reshape(n_chaos * cap, cells)
    my_fields = lax.dynamic_index_in_dim(windows[cap:], my_col_block, axis=2, keepdims=False)
    my_fields = my_fields.reshape(M + 1, cells)

    blocks, row_of, total = coupling_blocks(M)
    sizes, firsts, padded, offsets = degree_layout(M)
    coeff_of_row = np.full(total, -1, np.int64)
    coeff_of_row[row_of] = np.arange(count)
    row_coeff = jnp.asarray(np.maximum(coeff_of_row, 0), jnp.int32)
    group_ends = jnp.cumsum(lengths).astype(jnp.int32)
    group_starts = (group_ends - lengths).astype(jnp.int32)
    skipped = jnp.sum(
        jnp.where(row_coeff[:, None] >= group_ends[None, :], cap - lengths[None, :], 0), axis=1
    )
    slot_of_row = jnp.where(jnp.asarray(coeff_of_row >= 0), row_coeff + skipped, n_chaos * cap)
    by_slot = jnp.concatenate([by_slot, jnp.zeros((1, cells), jnp.float32)], axis=0)
    rhs = jnp.take(by_slot, slot_of_row, axis=0)

    row_at = my_row_block * rows - ghost + jnp.arange(patch_rows)
    col_at = my_col_block * width - ghost + jnp.arange(patch_cols)
    inside = ((row_at >= 0) & (row_at < rows * n_space))[:, None] & (
        (col_at >= 0) & (col_at < cols)
    )[None, :]
    inside = inside.reshape(cells)
    local_rows = jnp.arange(patch_rows)
    local_cols = jnp.arange(patch_cols)
    own = ((local_rows >= ghost) & (local_rows < ghost + rows))[:, None] & (
        (local_cols >= ghost) & (local_cols < ghost + width)
    )[None, :]
    own = own.reshape(cells)

    lanes = -(-cells // 128) * 128
    assert cells + patch_cols <= lanes
    rhs = jnp.pad(rhs, ((0, 0), (0, lanes - cells)))
    field_rows = -(-(M + 1) // 8) * 8
    field_in = jnp.pad(my_fields, ((0, field_rows - (M + 1)), (0, lanes - cells)))
    masks = jnp.stack([inside, own]).astype(jnp.float32)
    masks = jnp.pad(masks, ((0, 6), (0, lanes - cells)))
    mats = [jnp.asarray(blocks[d]) for d in range(4)]
    solved, partial_rows = pl.pallas_call(
        functools.partial(sweeps, padded=tuple(int(v) for v in padded), offsets=tuple(int(v) for v in offsets), cols=patch_cols),
        out_shape=(
            jax.ShapeDtypeStruct((total, lanes), jnp.float32),
            jax.ShapeDtypeStruct((8, 128), jnp.float32),
        ),
        in_specs=[pl.BlockSpec(memory_space=pltpu.VMEM)] * 7,
        out_specs=(pl.BlockSpec(memory_space=pltpu.VMEM), pl.BlockSpec(memory_space=pltpu.VMEM)),
        scratch_shapes=[pltpu.VMEM((M * padded[d], lanes), jnp.float32) for d in range(4)],
        compiler_params=pltpu.CompilerParams(vmem_limit_bytes=48 * 1024 * 1024),
    )(rhs, field_in, masks, *mats)
    partials = partial_rows[0, :ITERS]

    mine = solved[:, :cells].reshape(total, patch_rows, patch_cols)[
        :, ghost : ghost + rows, ghost : ghost + width
    ]
    mine = jnp.concatenate([mine, jnp.zeros((1, rows, width), jnp.float32)], axis=0)
    slot_index = jnp.arange(cap, dtype=jnp.int32)
    live = slot_index[None, :] < lengths[:, None]
    coeff = group_starts[:, None] + slot_index[None, :]
    shift = jnp.zeros_like(coeff)
    for d in range(1, 4):
        shift = jnp.where(coeff >= firsts[d], int(offsets[d] - firsts[d]), shift)
    row_of_slot = jnp.where(live, coeff + shift, total)
    by_slot_out = jnp.take(mine, row_of_slot.reshape(-1), axis=0)
    chunk = cap * rows * width
    payload = jnp.concatenate(
        [
            by_slot_out.reshape(n_chaos, chunk),
            jnp.broadcast_to(partials[None, :], (n_chaos, ITERS)),
        ],
        axis=1,
    )
    back = lax.all_to_all(payload, "chaos", 0, 0, tiled=True)
    out = back[:, :chunk].reshape(n_chaos, cap, rows, width)
    out = jnp.transpose(out, (1, 2, 0, 3)).reshape(cap, rows, cols)
    row_sum = jnp.sum(back[:, chunk:], axis=0)
    spread = jnp.broadcast_to(row_sum[None, :], (n_space, ITERS))
    all_rows = lax.all_to_all(spread, "space", 0, 0, tiled=True)
    norms = jnp.sqrt(jnp.sum(all_rows, axis=0))
    return (out, norms)


def solution(mesh):
    in_specs = (P("chaos", "space", None), P("space", None), P(None, "space", None), P())
    out_specs = (P("chaos", "space", None), P())
    return jax.shard_map(local, mesh=mesh, in_specs=in_specs, out_specs=out_specs, check_vma=False)
```

```python
import functools
import math

import jax
import jax.numpy as jnp
import numpy as np
from jax import lax
from jax.experimental import pallas as pl
from jax.experimental.pallas import tpu as pltpu
from jax.sharding import PartitionSpec as P

M = 12
P_SIZE = 455
ITERS = 3
GHOST = ITERS + 1


spectrum_low = 0.05
spectrum_high = 3.0


def index_key(entry):
    return tuple((int(value) for value in entry))


def chaos_tables(terms):
    indices = [np.zeros(terms, dtype=np.int64)]
    for first in range(terms):
        entry = np.zeros(terms, dtype=np.int64)
        entry[first] += 1
        indices.append(entry)
    for first in range(terms):
        for second in range(first, terms):
            entry = np.zeros(terms, dtype=np.int64)
            entry[first] += 1
            entry[second] += 1
            indices.append(entry)
    for first in range(terms):
        for second in range(first, terms):
            for third in range(second, terms):
                entry = np.zeros(terms, dtype=np.int64)
                entry[first] += 1
                entry[second] += 1
                entry[third] += 1
                indices.append(entry)
    lookup = {}
    for number, entry in enumerate(indices):
        lookup[index_key(entry)] = number
    count = len(indices)
    upward = np.full((count, terms), count, dtype=np.int64)
    downward = np.full((count, terms), count, dtype=np.int64)
    up_coef = np.zeros((count, terms))
    down_coef = np.zeros((count, terms))
    for number, entry in enumerate(indices):
        for term in range(terms):
            if entry.sum() < 3:
                other = entry.copy()
                other[term] += 1
                upward[number, term] = lookup[index_key(other)]
                up_coef[number, term] = math.sqrt(entry[term] + 1)
            if entry[term] > 0:
                other = entry.copy()
                other[term] -= 1
                downward[number, term] = lookup[index_key(other)]
                down_coef[number, term] = math.sqrt(entry[term])
    return (
        upward.astype(np.int32),
        downward.astype(np.int32),
        up_coef.astype(np.float32),
        down_coef.astype(np.float32),
    )


def degree_layout(terms):
    sizes = [1, terms, terms * (terms + 1) // 2, terms * (terms + 1) * (terms + 2) // 6]
    firsts = np.cumsum([0] + sizes[:-1])
    padded = [-(-size // 8) * 8 for size in sizes]
    offsets = np.cumsum([0] + padded[:-1])
    return sizes, firsts, padded, offsets


def coupling_blocks(terms):
    upward, downward, up_coef, down_coef = chaos_tables(terms)
    sizes, firsts, padded, offsets = degree_layout(terms)
    count = sum(sizes)
    total = sum(padded)
    row_of = np.zeros(count, np.int64)
    for d in range(4):
        row_of[firsts[d] : firsts[d] + sizes[d]] = offsets[d] + np.arange(sizes[d])
    dense = np.zeros((terms, total, total), np.float64)
    for p in range(count):
        for k in range(terms):
            if upward[p, k] < count:
                dense[k, row_of[p], row_of[upward[p, k]]] = up_coef[p, k]
            if downward[p, k] < count:
                dense[k, row_of[p], row_of[downward[p, k]]] = down_coef[p, k]

    def block(out_degrees, in_degree):
        rows = np.concatenate([offsets[d] + np.arange(padded[d]) for d in out_degrees])
        cols = offsets[in_degree] + np.arange(padded[in_degree])
        part = dense[:, rows][:, :, cols]
        return np.transpose(part, (1, 0, 2)).reshape(len(rows), terms * len(cols)).astype(np.float32)

    return {
        0: block((1,), 0),
        1: block((0, 2), 1),
        2: block((1, 3), 2),
        3: block((2,), 3),
    }, row_of, total


def neighbour(values, step):
    blank = jnp.zeros(values.shape[:-1] + (abs(step),), values.dtype)
    if step > 0:
        return jnp.concatenate([values[..., step:], blank], axis=-1)
    return jnp.concatenate([blank, values[..., :step]], axis=-1)


def exact_dot(left, right):
    return jnp.dot(left, right, precision=lax.Precision.HIGHEST, preferred_element_type=jnp.float32)


def sweeps(slots_ref, slot_of_row_ref, row_of_slot_ref, picks_ref, field_ref, mask_ref,
           w0_ref, w1_ref, w2_ref, w3_ref, out_ref, part_ref,
           s0_ref, s1_ref, s2_ref, s3_ref, *, padded, offsets, cols, state_rows):
    lanes = slots_ref.shape[1]
    total = slot_of_row_ref.shape[0]
    n_slots = slots_ref.shape[0]
    take = lax.broadcasted_iota(jnp.int32, (total, n_slots), 1) == slot_of_row_ref[...]
    rhs = exact_dot(take.astype(jnp.float32), slots_ref[...])
    shifts = (cols, lanes - cols, lanes - 1, 1)

    def near(values, shift):
        return pltpu.roll(values, shift, 1)

    fields = field_ref[...]
    inside = mask_ref[0:1, :] > 0.5
    own = mask_ref[1:2, :] > 0.5
    weights = [[0.5 * (fields[k : k + 1] + near(fields, s)[k : k + 1]) for s in shifts] for k in range(M + 1)]
    mean_now = fields[0:1]
    diagonal = 0.5 * (mean_now + near(mean_now, shifts[0]))
    for s in shifts[1:]:
        diagonal = diagonal + 0.5 * (mean_now + near(mean_now, s))
    diagonal = jnp.where(inside, diagonal, 1.0)
    stacks = (s0_ref, s1_ref, s2_ref, s3_ref)
    mats = (w0_ref, w1_ref, w2_ref, w3_ref)

    def operator(tiles):
        diffs = [tiles - near(tiles, s) for s in shifts]
        base = None
        for k in range(M + 1):
            term = weights[k][0] * diffs[0]
            for n in range(1, 4):
                term = term + weights[k][n] * diffs[n]
            if k == 0:
                base = term
                continue
            for d in range(4):
                stacks[d][(k - 1) * padded[d] : k * padded[d], :] = term[offsets[d] : offsets[d] + padded[d]]
        mixed = [
            exact_dot(mats[d][...], stacks[d][...])
            for d in range(4)
        ]
        p0, p1 = padded[0], padded[1]
        coupled = jnp.concatenate(
            [mixed[1][:p0], mixed[2][:p1] + mixed[0], mixed[3] + mixed[1][p0:], mixed[2][p1:]], axis=0
        )
        return base + coupled

    theta = (spectrum_high + spectrum_low) / 2.0
    delta = (spectrum_high - spectrum_low) / 2.0
    sigma = theta / delta
    rho = 1.0 / sigma
    residual = rhs
    solution = jnp.zeros_like(residual)
    direction = jnp.where(inside, residual / diagonal / theta, 0.0)
    lane = lax.broadcasted_iota(jnp.int32, (8, 128), 1)
    partial_out = jnp.zeros((8, 128), jnp.float32)
    for sweep_index in range(ITERS):
        solution = solution + direction
        residual = residual - operator(direction)
        value = jnp.sum(jnp.where(own, residual * residual, 0.0))
        partial_out = jnp.where(lane == sweep_index, value, partial_out)
        if sweep_index + 1 < ITERS:
            rho_new = 1.0 / (2.0 * sigma - rho)
            direction = rho_new * rho * direction + 2.0 * rho_new / delta * (residual / diagonal)
            direction = jnp.where(inside, direction, 0.0)
            rho = rho_new
    own_cells = exact_dot(solution, picks_ref[...])
    own_cells = jnp.concatenate(
        [own_cells, jnp.zeros((state_rows - total, own_cells.shape[1]), jnp.float32)], axis=0
    )
    put = lax.broadcasted_iota(jnp.int32, (n_slots, state_rows), 1) == row_of_slot_ref[...]
    out_ref[...] = exact_dot(put.astype(jnp.float32), own_cells)
    part_ref[...] = partial_out


def local(forcing, mean_field, modes, lengths):
    cap, rows, cols = forcing.shape
    n_space = lax.axis_size("space")
    n_chaos = lax.axis_size("chaos")
    my_row_block = lax.axis_index("space")
    my_col_block = lax.axis_index("chaos")
    width = cols // n_chaos
    ghost = GHOST
    assert rows >= ghost and ghost % width == 0 and width * n_chaos == cols
    patch_rows, patch_cols = rows + 2 * ghost, width + 2 * ghost
    cells = patch_rows * patch_cols
    count = P_SIZE

    fields = jnp.concatenate([mean_field[None], mean_field[None] * modes], axis=0)
    block = jnp.concatenate([forcing, fields], axis=0)
    down_pairs = [(i, i + 1) for i in range(n_space - 1)]
    up_pairs = [(i + 1, i) for i in range(n_space - 1)]
    above = lax.ppermute(block[:, rows - ghost :], "space", down_pairs)
    below = lax.ppermute(block[:, :ghost], "space", up_pairs)
    tall = jnp.concatenate([above, block, below], axis=1)
    tall = jnp.pad(tall, ((0, 0), (0, 0), (ghost, ghost)))

    side = ghost // width
    pieces = tall.reshape(tall.shape[0], patch_rows, n_chaos + 2 * side, width)
    windows = jnp.concatenate(
        [pieces[:, :, j : j + n_chaos] for j in range(2 * side + 1)], axis=-1
    )
    lanes = -(-cells // 128) * 128
    assert cells + patch_cols <= lanes
    slot_rows = -(-(cap + 1) // 8) * 8
    sent = jnp.transpose(windows[:cap], (2, 0, 1, 3)).reshape(n_chaos, cap, cells)
    sent = jnp.pad(sent, ((0, 0), (0, slot_rows - cap), (0, lanes - cells)))
    got = lax.all_to_all(sent, "chaos", 0, 0, tiled=True)
    by_slot = got.reshape(n_chaos * slot_rows, lanes)
    my_fields = lax.dynamic_index_in_dim(windows[cap:], my_col_block, axis=2, keepdims=False)
    my_fields = my_fields.reshape(M + 1, cells)

    blocks, row_of, total = coupling_blocks(M)
    sizes, firsts, padded, offsets = degree_layout(M)
    coeff_of_row = np.full(total, -1, np.int64)
    coeff_of_row[row_of] = np.arange(count)
    row_coeff = jnp.asarray(np.maximum(coeff_of_row, 0), jnp.int32)
    group_ends = jnp.cumsum(lengths).astype(jnp.int32)
    group_starts = (group_ends - lengths).astype(jnp.int32)
    skipped = jnp.sum(
        jnp.where(row_coeff[:, None] >= group_ends[None, :], slot_rows - lengths[None, :], 0), axis=1
    )
    slot_of_row = jnp.where(
        jnp.asarray(coeff_of_row >= 0), row_coeff + skipped, n_chaos * slot_rows - 1
    ).astype(jnp.int32)
    slot_index = jnp.arange(slot_rows, dtype=jnp.int32)
    live = slot_index[None, :] < lengths[:, None]
    coeff = group_starts[:, None] + slot_index[None, :]
    shift = jnp.zeros_like(coeff)
    for d in range(1, 4):
        shift = jnp.where(coeff >= firsts[d], int(offsets[d] - firsts[d]), shift)
    row_of_slot = jnp.where(live, coeff + shift, -1).astype(jnp.int32).reshape(-1)

    row_at = my_row_block * rows - ghost + jnp.arange(patch_rows)
    col_at = my_col_block * width - ghost + jnp.arange(patch_cols)
    inside = ((row_at >= 0) & (row_at < rows * n_space))[:, None] & (
        (col_at >= 0) & (col_at < cols)
    )[None, :]
    inside = inside.reshape(cells)
    local_rows = jnp.arange(patch_rows)
    local_cols = jnp.arange(patch_cols)
    own = ((local_rows >= ghost) & (local_rows < ghost + rows))[:, None] & (
        (local_cols >= ghost) & (local_cols < ghost + width)
    )[None, :]
    own = own.reshape(cells)

    field_rows = -(-(M + 1) // 8) * 8
    field_in = jnp.pad(my_fields, ((0, field_rows - (M + 1)), (0, lanes - cells)))
    masks = jnp.stack([inside, own]).astype(jnp.float32)
    masks = jnp.pad(masks, ((0, 6), (0, lanes - cells)))
    mats = [jnp.asarray(blocks[d]) for d in range(4)]
    own_lanes = np.flatnonzero(np.pad(np.ones((rows, width)), ghost).reshape(-1) > 0.5)
    picks = np.zeros((lanes, 128), np.float32)
    picks[own_lanes, np.arange(own_lanes.size)] = 1.0
    state_rows = -(-total // 128) * 128
    solved, partial_rows = pl.pallas_call(
        functools.partial(
            sweeps,
            padded=tuple(int(v) for v in padded),
            offsets=tuple(int(v) for v in offsets),
            cols=patch_cols,
            state_rows=state_rows,
        ),
        out_shape=(
            jax.ShapeDtypeStruct((n_chaos * slot_rows, 128), jnp.float32),
            jax.ShapeDtypeStruct((8, 128), jnp.float32),
        ),
        in_specs=[pl.BlockSpec(memory_space=pltpu.VMEM)] * 10,
        out_specs=(pl.BlockSpec(memory_space=pltpu.VMEM), pl.BlockSpec(memory_space=pltpu.VMEM)),
        scratch_shapes=[pltpu.VMEM((M * padded[d], lanes), jnp.float32) for d in range(4)],
        compiler_params=pltpu.CompilerParams(vmem_limit_bytes=48 * 1024 * 1024),
    )(by_slot, slot_of_row[:, None], row_of_slot[:, None], jnp.asarray(picks), field_in, masks, *mats)
    partials = partial_rows[0, :ITERS]

    own_count = rows * width
    by_slot_out = solved[:, :own_count].reshape(n_chaos, slot_rows, own_count)[:, :cap]
    chunk = cap * rows * width
    payload = jnp.concatenate(
        [
            by_slot_out.reshape(n_chaos, chunk),
            jnp.broadcast_to(partials[None, :], (n_chaos, ITERS)),
        ],
        axis=1,
    )
    back = lax.all_to_all(payload, "chaos", 0, 0, tiled=True)
    out = back[:, :chunk].reshape(n_chaos, cap, rows, width)
    out = jnp.transpose(out, (1, 2, 0, 3)).reshape(cap, rows, cols)
    row_sum = jnp.sum(back[:, chunk:], axis=0)
    spread = jnp.broadcast_to(row_sum[None, :], (n_space, ITERS))
    all_rows = lax.all_to_all(spread, "space", 0, 0, tiled=True)
    norms = jnp.sqrt(jnp.sum(all_rows, axis=0))
    return (out, norms)


def solution(mesh):
    in_specs = (P("chaos", "space", None), P("space", None), P(None, "space", None), P())
    out_specs = (P("chaos", "space", None), P())
    return jax.shard_map(local, mesh=mesh, in_specs=in_specs, out_specs=out_specs, check_vma=False)
```

```python
import functools
import math

import jax
import jax.numpy as jnp
import numpy as np
from jax import lax
from jax.experimental import pallas as pl
from jax.experimental.pallas import tpu as pltpu
from jax.sharding import PartitionSpec as P

M = 12
P_SIZE = 455
ITERS = 3
GHOST = ITERS
MOVED = ITERS + 1


spectrum_low = 0.05
spectrum_high = 3.0


def index_key(entry):
    return tuple((int(value) for value in entry))


def chaos_tables(terms):
    indices = [np.zeros(terms, dtype=np.int64)]
    for first in range(terms):
        entry = np.zeros(terms, dtype=np.int64)
        entry[first] += 1
        indices.append(entry)
    for first in range(terms):
        for second in range(first, terms):
            entry = np.zeros(terms, dtype=np.int64)
            entry[first] += 1
            entry[second] += 1
            indices.append(entry)
    for first in range(terms):
        for second in range(first, terms):
            for third in range(second, terms):
                entry = np.zeros(terms, dtype=np.int64)
                entry[first] += 1
                entry[second] += 1
                entry[third] += 1
                indices.append(entry)
    lookup = {}
    for number, entry in enumerate(indices):
        lookup[index_key(entry)] = number
    count = len(indices)
    upward = np.full((count, terms), count, dtype=np.int64)
    downward = np.full((count, terms), count, dtype=np.int64)
    up_coef = np.zeros((count, terms))
    down_coef = np.zeros((count, terms))
    for number, entry in enumerate(indices):
        for term in range(terms):
            if entry.sum() < 3:
                other = entry.copy()
                other[term] += 1
                upward[number, term] = lookup[index_key(other)]
                up_coef[number, term] = math.sqrt(entry[term] + 1)
            if entry[term] > 0:
                other = entry.copy()
                other[term] -= 1
                downward[number, term] = lookup[index_key(other)]
                down_coef[number, term] = math.sqrt(entry[term])
    return (
        upward.astype(np.int32),
        downward.astype(np.int32),
        up_coef.astype(np.float32),
        down_coef.astype(np.float32),
    )


def degree_layout(terms):
    sizes = [1, terms, terms * (terms + 1) // 2, terms * (terms + 1) * (terms + 2) // 6]
    firsts = np.cumsum([0] + sizes[:-1])
    padded = [-(-size // 8) * 8 for size in sizes]
    offsets = np.cumsum([0] + padded[:-1])
    return sizes, firsts, padded, offsets


def coupling_blocks(terms):
    upward, downward, up_coef, down_coef = chaos_tables(terms)
    sizes, firsts, padded, offsets = degree_layout(terms)
    count = sum(sizes)
    total = sum(padded)
    row_of = np.zeros(count, np.int64)
    for d in range(4):
        row_of[firsts[d] : firsts[d] + sizes[d]] = offsets[d] + np.arange(sizes[d])
    dense = np.zeros((terms, total, total), np.float64)
    for p in range(count):
        for k in range(terms):
            if upward[p, k] < count:
                dense[k, row_of[p], row_of[upward[p, k]]] = up_coef[p, k]
            if downward[p, k] < count:
                dense[k, row_of[p], row_of[downward[p, k]]] = down_coef[p, k]

    def block(out_degrees, in_degree):
        rows = np.concatenate([offsets[d] + np.arange(padded[d]) for d in out_degrees])
        cols = offsets[in_degree] + np.arange(padded[in_degree])
        part = dense[:, rows][:, :, cols]
        return np.transpose(part, (1, 0, 2)).reshape(len(rows), terms * len(cols)).astype(np.float32)

    return {
        0: block((1,), 0),
        1: block((0, 2), 1),
        2: block((1, 3), 2),
        3: block((2,), 3),
    }, row_of, total


def neighbour(values, step):
    blank = jnp.zeros(values.shape[:-1] + (abs(step),), values.dtype)
    if step > 0:
        return jnp.concatenate([values[..., step:], blank], axis=-1)
    return jnp.concatenate([blank, values[..., :step]], axis=-1)


def exact_dot(left, right):
    return jnp.dot(left, right, precision=lax.Precision.HIGHEST, preferred_element_type=jnp.float32)


def sweeps(slots_ref, slot_of_row_ref, row_of_slot_ref, picks_ref, field_ref, mask_ref,
           w0_ref, w1_ref, w2_ref, w3_ref, out_ref, part_ref,
           s0_ref, s1_ref, s2_ref, s3_ref, *, padded, offsets, cols, state_rows):
    lanes = slots_ref.shape[1]
    total = slot_of_row_ref.shape[0]
    n_slots = slots_ref.shape[0]
    take = lax.broadcasted_iota(jnp.int32, (total, n_slots), 1) == slot_of_row_ref[...]
    rhs = exact_dot(take.astype(jnp.float32), slots_ref[...])
    shifts = (cols, lanes - cols, lanes - 1, 1)

    def near(values, shift):
        return pltpu.roll(values, shift, 1)

    fields = field_ref[...]
    inside = mask_ref[0:1, :] > 0.5
    own = mask_ref[1:2, :] > 0.5
    weights = [[0.5 * (fields[k : k + 1] + near(fields, s)[k : k + 1]) for s in shifts] for k in range(M + 1)]
    diagonal = jnp.where(inside, mask_ref[2:3, :], 1.0)
    stacks = (s0_ref, s1_ref, s2_ref, s3_ref)
    mats = (w0_ref, w1_ref, w2_ref, w3_ref)

    def operator(tiles):
        diffs = [tiles - near(tiles, s) for s in shifts]
        base = None
        for k in range(M + 1):
            term = weights[k][0] * diffs[0]
            for n in range(1, 4):
                term = term + weights[k][n] * diffs[n]
            if k == 0:
                base = term
                continue
            for d in range(4):
                stacks[d][(k - 1) * padded[d] : k * padded[d], :] = term[offsets[d] : offsets[d] + padded[d]]
        mixed = [
            exact_dot(mats[d][...], stacks[d][...])
            for d in range(4)
        ]
        p0, p1 = padded[0], padded[1]
        coupled = jnp.concatenate(
            [mixed[1][:p0], mixed[2][:p1] + mixed[0], mixed[3] + mixed[1][p0:], mixed[2][p1:]], axis=0
        )
        return base + coupled

    theta = (spectrum_high + spectrum_low) / 2.0
    delta = (spectrum_high - spectrum_low) / 2.0
    sigma = theta / delta
    rho = 1.0 / sigma
    residual = rhs
    solution = jnp.zeros_like(residual)
    direction = jnp.where(inside, residual / diagonal / theta, 0.0)
    lane = lax.broadcasted_iota(jnp.int32, (8, 128), 1)
    partial_out = jnp.zeros((8, 128), jnp.float32)
    for sweep_index in range(ITERS):
        solution = solution + direction
        residual = residual - operator(direction)
        value = jnp.sum(jnp.where(own, residual * residual, 0.0))
        partial_out = jnp.where(lane == sweep_index, value, partial_out)
        if sweep_index + 1 < ITERS:
            rho_new = 1.0 / (2.0 * sigma - rho)
            direction = rho_new * rho * direction + 2.0 * rho_new / delta * (residual / diagonal)
            direction = jnp.where(inside, direction, 0.0)
            rho = rho_new
    own_cells = exact_dot(solution, picks_ref[...])
    own_cells = jnp.concatenate(
        [own_cells, jnp.zeros((state_rows - total, own_cells.shape[1]), jnp.float32)], axis=0
    )
    put = lax.broadcasted_iota(jnp.int32, (n_slots, state_rows), 1) == row_of_slot_ref[...]
    out_ref[...] = exact_dot(put.astype(jnp.float32), own_cells)
    part_ref[...] = partial_out


def local(forcing, mean_field, modes, lengths):
    cap, rows, cols = forcing.shape
    n_space = lax.axis_size("space")
    n_chaos = lax.axis_size("chaos")
    my_row_block = lax.axis_index("space")
    my_col_block = lax.axis_index("chaos")
    width = cols // n_chaos
    ghost, moved = GHOST, MOVED
    assert rows >= moved and moved % width == 0 and width * n_chaos == cols
    patch_rows, patch_cols = rows + 2 * ghost, width + 2 * ghost
    cells = patch_rows * patch_cols
    count = P_SIZE

    fields = jnp.concatenate([mean_field[None], mean_field[None] * modes], axis=0)
    block = jnp.concatenate([forcing, fields], axis=0)
    down_pairs = [(i, i + 1) for i in range(n_space - 1)]
    up_pairs = [(i + 1, i) for i in range(n_space - 1)]
    above = lax.ppermute(block[:, rows - moved :], "space", down_pairs)
    below = lax.ppermute(block[:, :moved], "space", up_pairs)
    tall = jnp.concatenate([above, block, below], axis=1)
    tall = jnp.pad(tall, ((0, 0), (0, 0), (moved, moved)))

    side = moved // width
    wide_rows = rows + 2 * moved
    pieces = tall.reshape(tall.shape[0], wide_rows, n_chaos + 2 * side, width)
    wide = jnp.concatenate(
        [pieces[:, :, j : j + n_chaos] for j in range(2 * side + 1)], axis=-1
    )
    trim = moved - ghost
    windows = wide[:, trim : wide_rows - trim, :, trim : width + 2 * moved - trim]
    lanes = -(-cells // 128) * 128
    assert cells + patch_cols <= lanes
    slot_rows = -(-(cap + 1) // 8) * 8
    sent = jnp.transpose(windows[:cap], (2, 0, 1, 3)).reshape(n_chaos, cap, cells)
    sent = jnp.pad(sent, ((0, 0), (0, slot_rows - cap), (0, lanes - cells)))
    got = lax.all_to_all(sent, "chaos", 0, 0, tiled=True)
    by_slot = got.reshape(n_chaos * slot_rows, lanes)
    my_fields = lax.dynamic_index_in_dim(windows[cap:], my_col_block, axis=2, keepdims=False)
    my_fields = my_fields.reshape(M + 1, cells)
    mean_wide = lax.dynamic_index_in_dim(wide[cap], my_col_block, axis=1, keepdims=False)
    mean_pad = jnp.pad(mean_wide, 1)
    centre = mean_pad[1:-1, 1:-1]
    diagonal = 0.5 * (centre + mean_pad[:-2, 1:-1])
    diagonal = diagonal + 0.5 * (centre + mean_pad[2:, 1:-1])
    diagonal = diagonal + 0.5 * (centre + mean_pad[1:-1, 2:])
    diagonal = diagonal + 0.5 * (centre + mean_pad[1:-1, :-2])
    diagonal = diagonal[trim : trim + patch_rows, trim : trim + patch_cols].reshape(cells)

    blocks, row_of, total = coupling_blocks(M)
    sizes, firsts, padded, offsets = degree_layout(M)
    coeff_of_row = np.full(total, -1, np.int64)
    coeff_of_row[row_of] = np.arange(count)
    row_coeff = jnp.asarray(np.maximum(coeff_of_row, 0), jnp.int32)
    group_ends = jnp.cumsum(lengths).astype(jnp.int32)
    group_starts = (group_ends - lengths).astype(jnp.int32)
    skipped = jnp.sum(
        jnp.where(row_coeff[:, None] >= group_ends[None, :], slot_rows - lengths[None, :], 0), axis=1
    )
    slot_of_row = jnp.where(
        jnp.asarray(coeff_of_row >= 0), row_coeff + skipped, n_chaos * slot_rows - 1
    ).astype(jnp.int32)
    slot_index = jnp.arange(slot_rows, dtype=jnp.int32)
    live = slot_index[None, :] < lengths[:, None]
    coeff = group_starts[:, None] + slot_index[None, :]
    shift = jnp.zeros_like(coeff)
    for d in range(1, 4):
        shift = jnp.where(coeff >= firsts[d], int(offsets[d] - firsts[d]), shift)
    row_of_slot = jnp.where(live, coeff + shift, -1).astype(jnp.int32).reshape(-1)

    row_at = my_row_block * rows - ghost + jnp.arange(patch_rows)
    col_at = my_col_block * width - ghost + jnp.arange(patch_cols)
    inside = ((row_at >= 0) & (row_at < rows * n_space))[:, None] & (
        (col_at >= 0) & (col_at < cols)
    )[None, :]
    inside = inside.reshape(cells)
    local_rows = jnp.arange(patch_rows)
    local_cols = jnp.arange(patch_cols)
    own = ((local_rows >= ghost) & (local_rows < ghost + rows))[:, None] & (
        (local_cols >= ghost) & (local_cols < ghost + width)
    )[None, :]
    own = own.reshape(cells)

    field_rows = -(-(M + 1) // 8) * 8
    field_in = jnp.pad(my_fields, ((0, field_rows - (M + 1)), (0, lanes - cells)))
    masks = jnp.stack([inside.astype(jnp.float32), own.astype(jnp.float32), diagonal])
    masks = jnp.pad(masks, ((0, 5), (0, lanes - cells)))
    mats = [jnp.asarray(blocks[d]) for d in range(4)]
    own_lanes = np.flatnonzero(np.pad(np.ones((rows, width)), ghost).reshape(-1) > 0.5)
    picks = np.zeros((lanes, 128), np.float32)
    picks[own_lanes, np.arange(own_lanes.size)] = 1.0
    state_rows = -(-total // 128) * 128
    solved, partial_rows = pl.pallas_call(
        functools.partial(
            sweeps,
            padded=tuple(int(v) for v in padded),
            offsets=tuple(int(v) for v in offsets),
            cols=patch_cols,
            state_rows=state_rows,
        ),
        out_shape=(
            jax.ShapeDtypeStruct((n_chaos * slot_rows, 128), jnp.float32),
            jax.ShapeDtypeStruct((8, 128), jnp.float32),
        ),
        in_specs=[pl.BlockSpec(memory_space=pltpu.VMEM)] * 10,
        out_specs=(pl.BlockSpec(memory_space=pltpu.VMEM), pl.BlockSpec(memory_space=pltpu.VMEM)),
        scratch_shapes=[pltpu.VMEM((M * padded[d], lanes), jnp.float32) for d in range(4)],
        compiler_params=pltpu.CompilerParams(vmem_limit_bytes=48 * 1024 * 1024),
    )(by_slot, slot_of_row[:, None], row_of_slot[:, None], jnp.asarray(picks), field_in, masks, *mats)
    partials = partial_rows[0, :ITERS]

    own_count = rows * width
    by_slot_out = solved[:, :own_count].reshape(n_chaos, slot_rows, own_count)[:, :cap]
    chunk = cap * rows * width
    payload = jnp.concatenate(
        [
            by_slot_out.reshape(n_chaos, chunk),
            jnp.broadcast_to(partials[None, :], (n_chaos, ITERS)),
        ],
        axis=1,
    )
    back = lax.all_to_all(payload, "chaos", 0, 0, tiled=True)
    out = back[:, :chunk].reshape(n_chaos, cap, rows, width)
    out = jnp.transpose(out, (1, 2, 0, 3)).reshape(cap, rows, cols)
    row_sum = jnp.sum(back[:, chunk:], axis=0)
    spread = jnp.broadcast_to(row_sum[None, :], (n_space, ITERS))
    all_rows = lax.all_to_all(spread, "space", 0, 0, tiled=True)
    norms = jnp.sqrt(jnp.sum(all_rows, axis=0))
    return (out, norms)


def solution(mesh):
    in_specs = (P("chaos", "space", None), P("space", None), P(None, "space", None), P())
    out_specs = (P("chaos", "space", None), P())
    return jax.shard_map(local, mesh=mesh, in_specs=in_specs, out_specs=out_specs, check_vma=False)
```

```python
import functools
import math

import jax
import jax.numpy as jnp
import numpy as np
from jax import lax
from jax.experimental import pallas as pl
from jax.experimental.pallas import tpu as pltpu
from jax.sharding import PartitionSpec as P

M = 12
P_SIZE = 455
ITERS = 3
GHOST = ITERS
MOVED = ITERS + 1


spectrum_low = 0.05
spectrum_high = 3.0


def index_key(entry):
    return tuple((int(value) for value in entry))


def chaos_tables(terms):
    indices = [np.zeros(terms, dtype=np.int64)]
    for first in range(terms):
        entry = np.zeros(terms, dtype=np.int64)
        entry[first] += 1
        indices.append(entry)
    for first in range(terms):
        for second in range(first, terms):
            entry = np.zeros(terms, dtype=np.int64)
            entry[first] += 1
            entry[second] += 1
            indices.append(entry)
    for first in range(terms):
        for second in range(first, terms):
            for third in range(second, terms):
                entry = np.zeros(terms, dtype=np.int64)
                entry[first] += 1
                entry[second] += 1
                entry[third] += 1
                indices.append(entry)
    lookup = {}
    for number, entry in enumerate(indices):
        lookup[index_key(entry)] = number
    count = len(indices)
    upward = np.full((count, terms), count, dtype=np.int64)
    downward = np.full((count, terms), count, dtype=np.int64)
    up_coef = np.zeros((count, terms))
    down_coef = np.zeros((count, terms))
    for number, entry in enumerate(indices):
        for term in range(terms):
            if entry.sum() < 3:
                other = entry.copy()
                other[term] += 1
                upward[number, term] = lookup[index_key(other)]
                up_coef[number, term] = math.sqrt(entry[term] + 1)
            if entry[term] > 0:
                other = entry.copy()
                other[term] -= 1
                downward[number, term] = lookup[index_key(other)]
                down_coef[number, term] = math.sqrt(entry[term])
    return (
        upward.astype(np.int32),
        downward.astype(np.int32),
        up_coef.astype(np.float32),
        down_coef.astype(np.float32),
    )


def degree_layout(terms):
    sizes = [1, terms, terms * (terms + 1) // 2, terms * (terms + 1) * (terms + 2) // 6]
    firsts = np.cumsum([0] + sizes[:-1])
    padded = [-(-size // 8) * 8 for size in sizes]
    offsets = np.cumsum([0] + padded[:-1])
    return sizes, firsts, padded, offsets


def coupling_blocks(terms):
    upward, downward, up_coef, down_coef = chaos_tables(terms)
    sizes, firsts, padded, offsets = degree_layout(terms)
    count = sum(sizes)
    total = sum(padded)
    row_of = np.zeros(count, np.int64)
    for d in range(4):
        row_of[firsts[d] : firsts[d] + sizes[d]] = offsets[d] + np.arange(sizes[d])
    dense = np.zeros((terms, total, total), np.float64)
    for p in range(count):
        for k in range(terms):
            if upward[p, k] < count:
                dense[k, row_of[p], row_of[upward[p, k]]] = up_coef[p, k]
            if downward[p, k] < count:
                dense[k, row_of[p], row_of[downward[p, k]]] = down_coef[p, k]

    def block(out_degrees, in_degree):
        rows = np.concatenate([offsets[d] + np.arange(padded[d]) for d in out_degrees])
        cols = offsets[in_degree] + np.arange(padded[in_degree])
        part = dense[:, rows][:, :, cols]
        return np.transpose(part, (1, 0, 2)).reshape(len(rows), terms * len(cols)).astype(np.float32)

    return {
        0: block((1,), 0),
        1: block((0, 2), 1),
        2: block((1, 3), 2),
        3: block((2,), 3),
    }, row_of, total


def neighbour(values, step):
    blank = jnp.zeros(values.shape[:-1] + (abs(step),), values.dtype)
    if step > 0:
        return jnp.concatenate([values[..., step:], blank], axis=-1)
    return jnp.concatenate([blank, values[..., :step]], axis=-1)


def exact_dot(left, right):
    return jnp.dot(left, right, precision=lax.Precision.HIGHEST, preferred_element_type=jnp.float32)


def sweeps(slots_ref, slot_of_row_ref, row_of_slot_ref, picks_ref, field_ref, mask_ref,
           w0_ref, w1_ref, w2_ref, w3_ref, out_ref, part_ref,
           s0_ref, s1_ref, s2_ref, s3_ref, *, padded, offsets, cols, state_rows):
    lanes = slots_ref.shape[1]
    total = slot_of_row_ref.shape[0]
    n_slots = slots_ref.shape[0]
    take = lax.broadcasted_iota(jnp.int32, (total, n_slots), 1) == slot_of_row_ref[...]
    rhs = exact_dot(take.astype(jnp.float32), slots_ref[...])
    shifts = (cols, lanes - cols, lanes - 1, 1)

    def near(values, shift):
        return pltpu.roll(values, shift, 1)

    fields = field_ref[...]
    inside = mask_ref[0:1, :] > 0.5
    own = mask_ref[1:2, :] > 0.5
    weights = [[0.5 * (fields[k : k + 1] + near(fields, s)[k : k + 1]) for s in shifts] for k in range(M + 1)]
    diagonal = jnp.where(inside, mask_ref[2:3, :], 1.0)
    stacks = (s0_ref, s1_ref, s2_ref, s3_ref)
    mats = (w0_ref, w1_ref, w2_ref, w3_ref)

    def operator(tiles):
        diffs = [tiles - near(tiles, s) for s in shifts]
        base = None
        for k in range(M + 1):
            term = weights[k][0] * diffs[0]
            for n in range(1, 4):
                term = term + weights[k][n] * diffs[n]
            if k == 0:
                base = term
                continue
            for d in range(4):
                stacks[d][(k - 1) * padded[d] : k * padded[d], :] = term[offsets[d] : offsets[d] + padded[d]]
        mixed = [
            exact_dot(mats[d][...], stacks[d][...])
            for d in range(4)
        ]
        p0, p1 = padded[0], padded[1]
        coupled = jnp.concatenate(
            [mixed[1][:p0], mixed[2][:p1] + mixed[0], mixed[3] + mixed[1][p0:], mixed[2][p1:]], axis=0
        )
        return base + coupled

    theta = (spectrum_high + spectrum_low) / 2.0
    delta = (spectrum_high - spectrum_low) / 2.0
    sigma = theta / delta
    rho = 1.0 / sigma
    residual = rhs
    solution = jnp.zeros_like(residual)
    direction = jnp.where(inside, residual / diagonal / theta, 0.0)
    lane = lax.broadcasted_iota(jnp.int32, (8, 128), 1)
    partial_out = jnp.zeros((8, 128), jnp.float32)
    for sweep_index in range(ITERS):
        solution = solution + direction
        residual = residual - operator(direction)
        value = jnp.sum(jnp.where(own, residual * residual, 0.0))
        partial_out = jnp.where(lane == sweep_index, value, partial_out)
        if sweep_index + 1 < ITERS:
            rho_new = 1.0 / (2.0 * sigma - rho)
            direction = rho_new * rho * direction + 2.0 * rho_new / delta * (residual / diagonal)
            direction = jnp.where(inside, direction, 0.0)
            rho = rho_new
    own_cells = exact_dot(solution, picks_ref[...])
    own_cells = jnp.concatenate(
        [own_cells, jnp.zeros((state_rows - total, own_cells.shape[1]), jnp.float32)], axis=0
    )
    put = lax.broadcasted_iota(jnp.int32, (n_slots, state_rows), 1) == row_of_slot_ref[...]
    out_ref[...] = exact_dot(put.astype(jnp.float32), own_cells)
    part_ref[...] = partial_out


def local(forcing, mean_field, modes, lengths):
    cap, rows, cols = forcing.shape
    n_space = lax.axis_size("space")
    n_chaos = lax.axis_size("chaos")
    my_row_block = lax.axis_index("space")
    my_col_block = lax.axis_index("chaos")
    width = cols // n_chaos
    ghost, moved = GHOST, MOVED
    assert rows >= moved and moved % width == 0 and width * n_chaos == cols
    patch_rows, patch_cols = rows + 2 * ghost, width + 2 * ghost
    cells = patch_rows * patch_cols
    count = P_SIZE

    fields = jnp.concatenate([mean_field[None], mean_field[None] * modes], axis=0)
    block = jnp.concatenate([forcing, fields], axis=0)
    down_pairs = [(i, i + 1) for i in range(n_space - 1)]
    up_pairs = [(i + 1, i) for i in range(n_space - 1)]
    above = lax.ppermute(block[:, rows - moved :], "space", down_pairs)
    below = lax.ppermute(block[:, :moved], "space", up_pairs)
    tall = jnp.concatenate([above, block, below], axis=1)
    tall = jnp.pad(tall, ((0, 0), (0, 0), (moved, moved)))

    side = moved // width
    wide_rows = rows + 2 * moved
    pieces = tall.reshape(tall.shape[0], wide_rows, n_chaos + 2 * side, width)
    wide = jnp.concatenate(
        [pieces[:, :, j : j + n_chaos] for j in range(2 * side + 1)], axis=-1
    )
    trim = moved - ghost
    windows = wide[:, trim : wide_rows - trim, :, trim : width + 2 * moved - trim]
    lanes = -(-cells // 128) * 128
    assert cells + patch_cols <= lanes
    slot_rows = -(-(cap + 1) // 8) * 8
    sent = jnp.transpose(windows[:cap], (2, 0, 1, 3)).reshape(n_chaos, cap, cells)
    sent = jnp.pad(sent, ((0, 0), (0, slot_rows - cap), (0, lanes - cells)))
    got = lax.all_to_all(sent, "chaos", 0, 0, tiled=True)
    by_slot = got.reshape(n_chaos * slot_rows, lanes)
    my_fields = lax.dynamic_index_in_dim(windows[cap:], my_col_block, axis=2, keepdims=False)
    my_fields = my_fields.reshape(M + 1, cells)
    mean_wide = lax.dynamic_index_in_dim(wide[cap], my_col_block, axis=1, keepdims=False)
    mean_pad = jnp.pad(mean_wide, 1)
    centre = mean_pad[1:-1, 1:-1]
    diagonal = 0.5 * (centre + mean_pad[:-2, 1:-1])
    diagonal = diagonal + 0.5 * (centre + mean_pad[2:, 1:-1])
    diagonal = diagonal + 0.5 * (centre + mean_pad[1:-1, 2:])
    diagonal = diagonal + 0.5 * (centre + mean_pad[1:-1, :-2])
    diagonal = diagonal[trim : trim + patch_rows, trim : trim + patch_cols].reshape(cells)

    blocks, row_of, total = coupling_blocks(M)
    sizes, firsts, padded, offsets = degree_layout(M)
    coeff_of_row = np.full(total, -1, np.int64)
    coeff_of_row[row_of] = np.arange(count)
    row_coeff = jnp.asarray(np.maximum(coeff_of_row, 0), jnp.int32)
    group_ends = jnp.cumsum(lengths).astype(jnp.int32)
    group_starts = (group_ends - lengths).astype(jnp.int32)
    skipped = jnp.sum(
        jnp.where(row_coeff[:, None] >= group_ends[None, :], slot_rows - lengths[None, :], 0), axis=1
    )
    slot_of_row = jnp.where(
        jnp.asarray(coeff_of_row >= 0), row_coeff + skipped, n_chaos * slot_rows - 1
    ).astype(jnp.int32)
    slot_index = jnp.arange(slot_rows, dtype=jnp.int32)
    live = slot_index[None, :] < lengths[:, None]
    coeff = group_starts[:, None] + slot_index[None, :]
    shift = jnp.zeros_like(coeff)
    for d in range(1, 4):
        shift = jnp.where(coeff >= firsts[d], int(offsets[d] - firsts[d]), shift)
    row_of_slot = jnp.where(live, coeff + shift, -1).astype(jnp.int32).reshape(-1)

    row_at = my_row_block * rows - ghost + jnp.arange(patch_rows)
    col_at = my_col_block * width - ghost + jnp.arange(patch_cols)
    inside = ((row_at >= 0) & (row_at < rows * n_space))[:, None] & (
        (col_at >= 0) & (col_at < cols)
    )[None, :]
    inside = inside.reshape(cells)
    local_rows = jnp.arange(patch_rows)
    local_cols = jnp.arange(patch_cols)
    own = ((local_rows >= ghost) & (local_rows < ghost + rows))[:, None] & (
        (local_cols >= ghost) & (local_cols < ghost + width)
    )[None, :]
    own = own.reshape(cells)

    field_rows = -(-(M + 1) // 8) * 8
    field_in = jnp.pad(my_fields, ((0, field_rows - (M + 1)), (0, lanes - cells)))
    masks = jnp.stack([inside.astype(jnp.float32), own.astype(jnp.float32), diagonal])
    masks = jnp.pad(masks, ((0, 5), (0, lanes - cells)))
    mats = []
    for d in range(4):
        height, wide_cols = blocks[d].shape
        part = blocks[d].reshape(height, M, wide_cols // M)
        assert np.all((part != 0).sum(axis=2) <= 1)
        partner = np.where(part.any(axis=2), part.argmax(axis=2), -1).astype(np.int32)
        value = part.max(axis=2).astype(np.float32)
        place = lax.broadcasted_iota(jnp.int32, part.shape, 2)
        built = jnp.where(
            place == jnp.asarray(partner)[:, :, None], jnp.asarray(value)[:, :, None], 0.0
        )
        mats.append(built.reshape(height, wide_cols))
    own_lanes = np.flatnonzero(np.pad(np.ones((rows, width)), ghost).reshape(-1) > 0.5)
    picks = np.zeros((lanes, 128), np.float32)
    picks[own_lanes, np.arange(own_lanes.size)] = 1.0
    state_rows = -(-total // 128) * 128
    solved, partial_rows = pl.pallas_call(
        functools.partial(
            sweeps,
            padded=tuple(int(v) for v in padded),
            offsets=tuple(int(v) for v in offsets),
            cols=patch_cols,
            state_rows=state_rows,
        ),
        out_shape=(
            jax.ShapeDtypeStruct((n_chaos * slot_rows, 128), jnp.float32),
            jax.ShapeDtypeStruct((8, 128), jnp.float32),
        ),
        in_specs=[pl.BlockSpec(memory_space=pltpu.VMEM)] * 10,
        out_specs=(pl.BlockSpec(memory_space=pltpu.VMEM), pl.BlockSpec(memory_space=pltpu.VMEM)),
        scratch_shapes=[pltpu.VMEM((M * padded[d], lanes), jnp.float32) for d in range(4)],
        compiler_params=pltpu.CompilerParams(vmem_limit_bytes=48 * 1024 * 1024),
    )(by_slot, slot_of_row[:, None], row_of_slot[:, None], jnp.asarray(picks), field_in, masks, *mats)
    partials = partial_rows[0, :ITERS]

    own_count = rows * width
    by_slot_out = solved[:, :own_count].reshape(n_chaos, slot_rows, own_count)[:, :cap]
    chunk = cap * rows * width
    payload = jnp.concatenate(
        [
            by_slot_out.reshape(n_chaos, chunk),
            jnp.broadcast_to(partials[None, :], (n_chaos, ITERS)),
        ],
        axis=1,
    )
    back = lax.all_to_all(payload, "chaos", 0, 0, tiled=True)
    out = back[:, :chunk].reshape(n_chaos, cap, rows, width)
    out = jnp.transpose(out, (1, 2, 0, 3)).reshape(cap, rows, cols)
    row_sum = jnp.sum(back[:, chunk:], axis=0)
    spread = jnp.broadcast_to(row_sum[None, :], (n_space, ITERS))
    all_rows = lax.all_to_all(spread, "space", 0, 0, tiled=True)
    norms = jnp.sqrt(jnp.sum(all_rows, axis=0))
    return (out, norms)


def solution(mesh):
    in_specs = (P("chaos", "space", None), P("space", None), P(None, "space", None), P())
    out_specs = (P("chaos", "space", None), P())
    return jax.shard_map(local, mesh=mesh, in_specs=in_specs, out_specs=out_specs, check_vma=False)
```

```python
import functools
import math

import jax
import jax.numpy as jnp
import numpy as np
from jax import lax
from jax.experimental import pallas as pl
from jax.experimental.pallas import tpu as pltpu
from jax.sharding import PartitionSpec as P

M = 12
P_SIZE = 455
ITERS = 3
GHOST = ITERS
MOVED = ITERS + 1


spectrum_low = 0.05
spectrum_high = 3.0


def index_key(entry):
    return tuple((int(value) for value in entry))


def chaos_tables(terms):
    indices = [np.zeros(terms, dtype=np.int64)]
    for first in range(terms):
        entry = np.zeros(terms, dtype=np.int64)
        entry[first] += 1
        indices.append(entry)
    for first in range(terms):
        for second in range(first, terms):
            entry = np.zeros(terms, dtype=np.int64)
            entry[first] += 1
            entry[second] += 1
            indices.append(entry)
    for first in range(terms):
        for second in range(first, terms):
            for third in range(second, terms):
                entry = np.zeros(terms, dtype=np.int64)
                entry[first] += 1
                entry[second] += 1
                entry[third] += 1
                indices.append(entry)
    lookup = {}
    for number, entry in enumerate(indices):
        lookup[index_key(entry)] = number
    count = len(indices)
    upward = np.full((count, terms), count, dtype=np.int64)
    downward = np.full((count, terms), count, dtype=np.int64)
    up_coef = np.zeros((count, terms))
    down_coef = np.zeros((count, terms))
    for number, entry in enumerate(indices):
        for term in range(terms):
            if entry.sum() < 3:
                other = entry.copy()
                other[term] += 1
                upward[number, term] = lookup[index_key(other)]
                up_coef[number, term] = math.sqrt(entry[term] + 1)
            if entry[term] > 0:
                other = entry.copy()
                other[term] -= 1
                downward[number, term] = lookup[index_key(other)]
                down_coef[number, term] = math.sqrt(entry[term])
    return (
        upward.astype(np.int32),
        downward.astype(np.int32),
        up_coef.astype(np.float32),
        down_coef.astype(np.float32),
    )


def degree_layout(terms):
    sizes = [1, terms, terms * (terms + 1) // 2, terms * (terms + 1) * (terms + 2) // 6]
    firsts = np.cumsum([0] + sizes[:-1])
    padded = [-(-size // 8) * 8 for size in sizes]
    offsets = np.cumsum([0] + padded[:-1])
    return sizes, firsts, padded, offsets


def coupling_blocks(terms):
    upward, downward, up_coef, down_coef = chaos_tables(terms)
    sizes, firsts, padded, offsets = degree_layout(terms)
    count = sum(sizes)
    total = sum(padded)
    row_of = np.zeros(count, np.int64)
    for d in range(4):
        row_of[firsts[d] : firsts[d] + sizes[d]] = offsets[d] + np.arange(sizes[d])
    dense = np.zeros((terms, total, total), np.float64)
    for p in range(count):
        for k in range(terms):
            if upward[p, k] < count:
                dense[k, row_of[p], row_of[upward[p, k]]] = up_coef[p, k]
            if downward[p, k] < count:
                dense[k, row_of[p], row_of[downward[p, k]]] = down_coef[p, k]

    def block(out_degrees, in_degree):
        rows = np.concatenate([offsets[d] + np.arange(padded[d]) for d in out_degrees])
        cols = offsets[in_degree] + np.arange(padded[in_degree])
        part = dense[:, rows][:, :, cols]
        return np.transpose(part, (1, 0, 2)).reshape(len(rows), terms * len(cols)).astype(np.float32)

    return {
        0: block((1,), 0),
        1: block((0, 2), 1),
        2: block((1, 3), 2),
        3: block((2,), 3),
    }, row_of, total


def neighbour(values, step):
    blank = jnp.zeros(values.shape[:-1] + (abs(step),), values.dtype)
    if step > 0:
        return jnp.concatenate([values[..., step:], blank], axis=-1)
    return jnp.concatenate([blank, values[..., :step]], axis=-1)


def exact_dot(left, right):
    return jnp.dot(left, right, precision=lax.Precision.HIGHEST, preferred_element_type=jnp.float32)


def sweeps(slots_ref, slot_of_row_ref, row_of_slot_ref, picks_ref, field_ref, mask_ref,
           w0_ref, w1_ref, w2_ref, w3_ref, out_ref, part_ref,
           s0_ref, s1_ref, s2_ref, s3_ref, *, padded, offsets, cols, state_rows):
    lanes = slots_ref.shape[1]
    total = slot_of_row_ref.shape[0]
    n_slots = slots_ref.shape[0]
    take = lax.broadcasted_iota(jnp.int32, (total, n_slots), 1) == slot_of_row_ref[...]
    rhs = exact_dot(take.astype(jnp.float32), slots_ref[...])
    shifts = (cols, lanes - cols, lanes - 1, 1)

    def near(values, shift):
        return pltpu.roll(values, shift, 1)

    fields = field_ref[...]
    inside = mask_ref[0:1, :] > 0.5
    own = mask_ref[1:2, :] > 0.5
    weights = [[0.5 * (fields[k : k + 1] + near(fields, s)[k : k + 1]) for s in shifts] for k in range(M + 1)]
    diagonal = jnp.where(inside, mask_ref[2:3, :], 1.0)
    stacks = (s0_ref, s1_ref, s2_ref, s3_ref)
    mats = (w0_ref, w1_ref, w2_ref, w3_ref)

    def operator(tiles):
        diffs = [tiles - near(tiles, s) for s in shifts]
        base = None
        for k in range(M + 1):
            term = weights[k][0] * diffs[0]
            for n in range(1, 4):
                term = term + weights[k][n] * diffs[n]
            if k == 0:
                base = term
                continue
            for d in range(4):
                stacks[d][(k - 1) * padded[d] : k * padded[d], :] = term[offsets[d] : offsets[d] + padded[d]]
        mixed = [
            jnp.dot(
                mats[d][...],
                stacks[d][...],
                precision=lax.Precision.HIGH,
                preferred_element_type=jnp.float32,
            )
            for d in range(4)
        ]
        p0, p1 = padded[0], padded[1]
        coupled = jnp.concatenate(
            [mixed[1][:p0], mixed[2][:p1] + mixed[0], mixed[3] + mixed[1][p0:], mixed[2][p1:]], axis=0
        )
        return base + coupled

    theta = (spectrum_high + spectrum_low) / 2.0
    delta = (spectrum_high - spectrum_low) / 2.0
    sigma = theta / delta
    rho = 1.0 / sigma
    residual = rhs
    solution = jnp.zeros_like(residual)
    direction = jnp.where(inside, residual / diagonal / theta, 0.0)
    lane = lax.broadcasted_iota(jnp.int32, (8, 128), 1)
    partial_out = jnp.zeros((8, 128), jnp.float32)
    for sweep_index in range(ITERS):
        solution = solution + direction
        residual = residual - operator(direction)
        value = jnp.sum(jnp.where(own, residual * residual, 0.0))
        partial_out = jnp.where(lane == sweep_index, value, partial_out)
        if sweep_index + 1 < ITERS:
            rho_new = 1.0 / (2.0 * sigma - rho)
            direction = rho_new * rho * direction + 2.0 * rho_new / delta * (residual / diagonal)
            direction = jnp.where(inside, direction, 0.0)
            rho = rho_new
    own_cells = exact_dot(solution, picks_ref[...])
    own_cells = jnp.concatenate(
        [own_cells, jnp.zeros((state_rows - total, own_cells.shape[1]), jnp.float32)], axis=0
    )
    put = lax.broadcasted_iota(jnp.int32, (n_slots, state_rows), 1) == row_of_slot_ref[...]
    out_ref[...] = exact_dot(put.astype(jnp.float32), own_cells)
    part_ref[...] = partial_out


def local(forcing, mean_field, modes, lengths):
    cap, rows, cols = forcing.shape
    n_space = lax.axis_size("space")
    n_chaos = lax.axis_size("chaos")
    my_row_block = lax.axis_index("space")
    my_col_block = lax.axis_index("chaos")
    width = cols // n_chaos
    ghost, moved = GHOST, MOVED
    assert rows >= moved and moved % width == 0 and width * n_chaos == cols
    patch_rows, patch_cols = rows + 2 * ghost, width + 2 * ghost
    cells = patch_rows * patch_cols
    count = P_SIZE

    fields = jnp.concatenate([mean_field[None], mean_field[None] * modes], axis=0)
    block = jnp.concatenate([forcing, fields], axis=0)
    down_pairs = [(i, i + 1) for i in range(n_space - 1)]
    up_pairs = [(i + 1, i) for i in range(n_space - 1)]
    above = lax.ppermute(block[:, rows - moved :], "space", down_pairs)
    below = lax.ppermute(block[:, :moved], "space", up_pairs)
    tall = jnp.concatenate([above, block, below], axis=1)
    tall = jnp.pad(tall, ((0, 0), (0, 0), (moved, moved)))

    side = moved // width
    wide_rows = rows + 2 * moved
    pieces = tall.reshape(tall.shape[0], wide_rows, n_chaos + 2 * side, width)
    wide = jnp.concatenate(
        [pieces[:, :, j : j + n_chaos] for j in range(2 * side + 1)], axis=-1
    )
    trim = moved - ghost
    windows = wide[:, trim : wide_rows - trim, :, trim : width + 2 * moved - trim]
    lanes = -(-cells // 128) * 128
    assert cells + patch_cols <= lanes
    slot_rows = -(-(cap + 1) // 8) * 8
    sent = jnp.transpose(windows[:cap], (2, 0, 1, 3)).reshape(n_chaos, cap, cells)
    sent = jnp.pad(sent, ((0, 0), (0, slot_rows - cap), (0, lanes - cells)))
    got = lax.all_to_all(sent, "chaos", 0, 0, tiled=True)
    by_slot = got.reshape(n_chaos * slot_rows, lanes)
    my_fields = lax.dynamic_index_in_dim(windows[cap:], my_col_block, axis=2, keepdims=False)
    my_fields = my_fields.reshape(M + 1, cells)
    mean_wide = lax.dynamic_index_in_dim(wide[cap], my_col_block, axis=1, keepdims=False)
    mean_pad = jnp.pad(mean_wide, 1)
    centre = mean_pad[1:-1, 1:-1]
    diagonal = 0.5 * (centre + mean_pad[:-2, 1:-1])
    diagonal = diagonal + 0.5 * (centre + mean_pad[2:, 1:-1])
    diagonal = diagonal + 0.5 * (centre + mean_pad[1:-1, 2:])
    diagonal = diagonal + 0.5 * (centre + mean_pad[1:-1, :-2])
    diagonal = diagonal[trim : trim + patch_rows, trim : trim + patch_cols].reshape(cells)

    blocks, row_of, total = coupling_blocks(M)
    sizes, firsts, padded, offsets = degree_layout(M)
    coeff_of_row = np.full(total, -1, np.int64)
    coeff_of_row[row_of] = np.arange(count)
    row_coeff = jnp.asarray(np.maximum(coeff_of_row, 0), jnp.int32)
    group_ends = jnp.cumsum(lengths).astype(jnp.int32)
    group_starts = (group_ends - lengths).astype(jnp.int32)
    skipped = jnp.sum(
        jnp.where(row_coeff[:, None] >= group_ends[None, :], slot_rows - lengths[None, :], 0), axis=1
    )
    slot_of_row = jnp.where(
        jnp.asarray(coeff_of_row >= 0), row_coeff + skipped, n_chaos * slot_rows - 1
    ).astype(jnp.int32)
    slot_index = jnp.arange(slot_rows, dtype=jnp.int32)
    live = slot_index[None, :] < lengths[:, None]
    coeff = group_starts[:, None] + slot_index[None, :]
    shift = jnp.zeros_like(coeff)
    for d in range(1, 4):
        shift = jnp.where(coeff >= firsts[d], int(offsets[d] - firsts[d]), shift)
    row_of_slot = jnp.where(live, coeff + shift, -1).astype(jnp.int32).reshape(-1)

    row_at = my_row_block * rows - ghost + jnp.arange(patch_rows)
    col_at = my_col_block * width - ghost + jnp.arange(patch_cols)
    inside = ((row_at >= 0) & (row_at < rows * n_space))[:, None] & (
        (col_at >= 0) & (col_at < cols)
    )[None, :]
    inside = inside.reshape(cells)
    local_rows = jnp.arange(patch_rows)
    local_cols = jnp.arange(patch_cols)
    own = ((local_rows >= ghost) & (local_rows < ghost + rows))[:, None] & (
        (local_cols >= ghost) & (local_cols < ghost + width)
    )[None, :]
    own = own.reshape(cells)

    field_rows = -(-(M + 1) // 8) * 8
    field_in = jnp.pad(my_fields, ((0, field_rows - (M + 1)), (0, lanes - cells)))
    masks = jnp.stack([inside.astype(jnp.float32), own.astype(jnp.float32), diagonal])
    masks = jnp.pad(masks, ((0, 5), (0, lanes - cells)))
    mats = [jnp.asarray(blocks[d]) for d in range(4)]
    own_lanes = np.flatnonzero(np.pad(np.ones((rows, width)), ghost).reshape(-1) > 0.5)
    picks = np.zeros((lanes, 128), np.float32)
    picks[own_lanes, np.arange(own_lanes.size)] = 1.0
    state_rows = -(-total // 128) * 128
    solved, partial_rows = pl.pallas_call(
        functools.partial(
            sweeps,
            padded=tuple(int(v) for v in padded),
            offsets=tuple(int(v) for v in offsets),
            cols=patch_cols,
            state_rows=state_rows,
        ),
        out_shape=(
            jax.ShapeDtypeStruct((n_chaos * slot_rows, 128), jnp.float32),
            jax.ShapeDtypeStruct((8, 128), jnp.float32),
        ),
        in_specs=[pl.BlockSpec(memory_space=pltpu.VMEM)] * 10,
        out_specs=(pl.BlockSpec(memory_space=pltpu.VMEM), pl.BlockSpec(memory_space=pltpu.VMEM)),
        scratch_shapes=[pltpu.VMEM((M * padded[d], lanes), jnp.float32) for d in range(4)],
        compiler_params=pltpu.CompilerParams(vmem_limit_bytes=48 * 1024 * 1024),
    )(by_slot, slot_of_row[:, None], row_of_slot[:, None], jnp.asarray(picks), field_in, masks, *mats)
    partials = partial_rows[0, :ITERS]

    own_count = rows * width
    by_slot_out = solved[:, :own_count].reshape(n_chaos, slot_rows, own_count)[:, :cap]
    chunk = cap * rows * width
    payload = jnp.concatenate(
        [
            by_slot_out.reshape(n_chaos, chunk),
            jnp.broadcast_to(partials[None, :], (n_chaos, ITERS)),
        ],
        axis=1,
    )
    back = lax.all_to_all(payload, "chaos", 0, 0, tiled=True)
    out = back[:, :chunk].reshape(n_chaos, cap, rows, width)
    out = jnp.transpose(out, (1, 2, 0, 3)).reshape(cap, rows, cols)
    row_sum = jnp.sum(back[:, chunk:], axis=0)
    spread = jnp.broadcast_to(row_sum[None, :], (n_space, ITERS))
    all_rows = lax.all_to_all(spread, "space", 0, 0, tiled=True)
    norms = jnp.sqrt(jnp.sum(all_rows, axis=0))
    return (out, norms)


def solution(mesh):
    in_specs = (P("chaos", "space", None), P("space", None), P(None, "space", None), P())
    out_specs = (P("chaos", "space", None), P())
    return jax.shard_map(local, mesh=mesh, in_specs=in_specs, out_specs=out_specs, check_vma=False)
```

```python
import functools
import math

import jax
import jax.numpy as jnp
import numpy as np
from jax import lax
from jax.experimental import pallas as pl
from jax.experimental.pallas import tpu as pltpu
from jax.sharding import PartitionSpec as P

M = 12
P_SIZE = 455
ITERS = 3
GHOST = ITERS
MOVED = ITERS + 1


spectrum_low = 0.05
spectrum_high = 3.0


def index_key(entry):
    return tuple((int(value) for value in entry))


def chaos_tables(terms):
    indices = [np.zeros(terms, dtype=np.int64)]
    for first in range(terms):
        entry = np.zeros(terms, dtype=np.int64)
        entry[first] += 1
        indices.append(entry)
    for first in range(terms):
        for second in range(first, terms):
            entry = np.zeros(terms, dtype=np.int64)
            entry[first] += 1
            entry[second] += 1
            indices.append(entry)
    for first in range(terms):
        for second in range(first, terms):
            for third in range(second, terms):
                entry = np.zeros(terms, dtype=np.int64)
                entry[first] += 1
                entry[second] += 1
                entry[third] += 1
                indices.append(entry)
    lookup = {}
    for number, entry in enumerate(indices):
        lookup[index_key(entry)] = number
    count = len(indices)
    upward = np.full((count, terms), count, dtype=np.int64)
    downward = np.full((count, terms), count, dtype=np.int64)
    up_coef = np.zeros((count, terms))
    down_coef = np.zeros((count, terms))
    for number, entry in enumerate(indices):
        for term in range(terms):
            if entry.sum() < 3:
                other = entry.copy()
                other[term] += 1
                upward[number, term] = lookup[index_key(other)]
                up_coef[number, term] = math.sqrt(entry[term] + 1)
            if entry[term] > 0:
                other = entry.copy()
                other[term] -= 1
                downward[number, term] = lookup[index_key(other)]
                down_coef[number, term] = math.sqrt(entry[term])
    return (
        upward.astype(np.int32),
        downward.astype(np.int32),
        up_coef.astype(np.float32),
        down_coef.astype(np.float32),
    )


def degree_layout(terms):
    sizes = [1, terms, terms * (terms + 1) // 2, terms * (terms + 1) * (terms + 2) // 6]
    firsts = np.cumsum([0] + sizes[:-1])
    padded = [-(-size // 8) * 8 for size in sizes]
    offsets = np.cumsum([0] + padded[:-1])
    return sizes, firsts, padded, offsets


def coupling_blocks(terms):
    upward, downward, up_coef, down_coef = chaos_tables(terms)
    sizes, firsts, padded, offsets = degree_layout(terms)
    count = sum(sizes)
    total = sum(padded)
    row_of = np.zeros(count, np.int64)
    for d in range(4):
        row_of[firsts[d] : firsts[d] + sizes[d]] = offsets[d] + np.arange(sizes[d])
    dense = np.zeros((terms, total, total), np.float64)
    for p in range(count):
        for k in range(terms):
            if upward[p, k] < count:
                dense[k, row_of[p], row_of[upward[p, k]]] = up_coef[p, k]
            if downward[p, k] < count:
                dense[k, row_of[p], row_of[downward[p, k]]] = down_coef[p, k]

    def block(out_degrees, in_degree):
        rows = np.concatenate([offsets[d] + np.arange(padded[d]) for d in out_degrees])
        cols = offsets[in_degree] + np.arange(padded[in_degree])
        part = dense[:, rows][:, :, cols]
        return np.transpose(part, (1, 0, 2)).reshape(len(rows), terms * len(cols)).astype(np.float32)

    return {
        0: block((1,), 0),
        1: block((0, 2), 1),
        2: block((1, 3), 2),
        3: block((2,), 3),
    }, row_of, total


def neighbour(values, step):
    blank = jnp.zeros(values.shape[:-1] + (abs(step),), values.dtype)
    if step > 0:
        return jnp.concatenate([values[..., step:], blank], axis=-1)
    return jnp.concatenate([blank, values[..., :step]], axis=-1)


def exact_dot(left, right):
    return jnp.dot(left, right, precision=lax.Precision.HIGHEST, preferred_element_type=jnp.float32)


def pick_dot(left, right, split_left):
    ones, values = (right, left) if split_left else (left, right)
    ones = ones.astype(jnp.bfloat16)
    high = values.astype(jnp.bfloat16)
    rest = values - high.astype(jnp.float32)
    middle = rest.astype(jnp.bfloat16)
    low = (rest - middle.astype(jnp.float32)).astype(jnp.bfloat16)
    total = None
    for part in (high, middle, low):
        pair = (part, ones) if split_left else (ones, part)
        step = jnp.dot(*pair, preferred_element_type=jnp.float32)
        total = step if total is None else total + step
    return total


def sweeps(slots_ref, slot_of_row_ref, row_of_slot_ref, picks_ref, field_ref, mask_ref,
           w0_ref, w1_ref, w2_ref, w3_ref, out_ref, part_ref,
           s0_ref, s1_ref, s2_ref, s3_ref, *, padded, offsets, cols, state_rows):
    lanes = slots_ref.shape[1]
    total = slot_of_row_ref.shape[0]
    n_slots = slots_ref.shape[0]
    take = lax.broadcasted_iota(jnp.int32, (total, n_slots), 1) == slot_of_row_ref[...]
    rhs = pick_dot(take.astype(jnp.float32), slots_ref[...], False)
    shifts = (cols, lanes - cols, lanes - 1, 1)

    def near(values, shift):
        return pltpu.roll(values, shift, 1)

    fields = field_ref[...]
    inside = mask_ref[0:1, :] > 0.5
    own = mask_ref[1:2, :] > 0.5
    weights = [[0.5 * (fields[k : k + 1] + near(fields, s)[k : k + 1]) for s in shifts] for k in range(M + 1)]
    diagonal = jnp.where(inside, mask_ref[2:3, :], 1.0)
    stacks = (s0_ref, s1_ref, s2_ref, s3_ref)
    mats = (w0_ref, w1_ref, w2_ref, w3_ref)

    def operator(tiles):
        diffs = [tiles - near(tiles, s) for s in shifts]
        base = None
        for k in range(M + 1):
            term = weights[k][0] * diffs[0]
            for n in range(1, 4):
                term = term + weights[k][n] * diffs[n]
            if k == 0:
                base = term
                continue
            for d in range(4):
                stacks[d][(k - 1) * padded[d] : k * padded[d], :] = term[offsets[d] : offsets[d] + padded[d]]
        mixed = [
            jnp.dot(
                mats[d][...],
                stacks[d][...],
                precision=lax.Precision.HIGH,
                preferred_element_type=jnp.float32,
            )
            for d in range(4)
        ]
        p0, p1 = padded[0], padded[1]
        coupled = jnp.concatenate(
            [mixed[1][:p0], mixed[2][:p1] + mixed[0], mixed[3] + mixed[1][p0:], mixed[2][p1:]], axis=0
        )
        return base + coupled

    theta = (spectrum_high + spectrum_low) / 2.0
    delta = (spectrum_high - spectrum_low) / 2.0
    sigma = theta / delta
    rho = 1.0 / sigma
    residual = rhs
    solution = jnp.zeros_like(residual)
    direction = jnp.where(inside, residual / diagonal / theta, 0.0)
    lane = lax.broadcasted_iota(jnp.int32, (8, 128), 1)
    partial_out = jnp.zeros((8, 128), jnp.float32)
    for sweep_index in range(ITERS):
        solution = solution + direction
        residual = residual - operator(direction)
        value = jnp.sum(jnp.where(own, residual * residual, 0.0))
        partial_out = jnp.where(lane == sweep_index, value, partial_out)
        if sweep_index + 1 < ITERS:
            rho_new = 1.0 / (2.0 * sigma - rho)
            direction = rho_new * rho * direction + 2.0 * rho_new / delta * (residual / diagonal)
            direction = jnp.where(inside, direction, 0.0)
            rho = rho_new
    own_cells = pick_dot(solution, picks_ref[...], True)
    own_cells = jnp.concatenate(
        [own_cells, jnp.zeros((state_rows - total, own_cells.shape[1]), jnp.float32)], axis=0
    )
    put = lax.broadcasted_iota(jnp.int32, (n_slots, state_rows), 1) == row_of_slot_ref[...]
    out_ref[...] = pick_dot(put.astype(jnp.float32), own_cells, False)
    part_ref[...] = partial_out


def local(forcing, mean_field, modes, lengths):
    cap, rows, cols = forcing.shape
    n_space = lax.axis_size("space")
    n_chaos = lax.axis_size("chaos")
    my_row_block = lax.axis_index("space")
    my_col_block = lax.axis_index("chaos")
    width = cols // n_chaos
    ghost, moved = GHOST, MOVED
    assert rows >= moved and moved % width == 0 and width * n_chaos == cols
    patch_rows, patch_cols = rows + 2 * ghost, width + 2 * ghost
    cells = patch_rows * patch_cols
    count = P_SIZE

    fields = jnp.concatenate([mean_field[None], mean_field[None] * modes], axis=0)
    block = jnp.concatenate([forcing, fields], axis=0)
    down_pairs = [(i, i + 1) for i in range(n_space - 1)]
    up_pairs = [(i + 1, i) for i in range(n_space - 1)]
    above = lax.ppermute(block[:, rows - moved :], "space", down_pairs)
    below = lax.ppermute(block[:, :moved], "space", up_pairs)
    tall = jnp.concatenate([above, block, below], axis=1)
    tall = jnp.pad(tall, ((0, 0), (0, 0), (moved, moved)))

    side = moved // width
    wide_rows = rows + 2 * moved
    pieces = tall.reshape(tall.shape[0], wide_rows, n_chaos + 2 * side, width)
    wide = jnp.concatenate(
        [pieces[:, :, j : j + n_chaos] for j in range(2 * side + 1)], axis=-1
    )
    trim = moved - ghost
    windows = wide[:, trim : wide_rows - trim, :, trim : width + 2 * moved - trim]
    lanes = -(-cells // 128) * 128
    assert cells + patch_cols <= lanes
    slot_rows = -(-(cap + 1) // 8) * 8
    sent = jnp.transpose(windows[:cap], (2, 0, 1, 3)).reshape(n_chaos, cap, cells)
    sent = jnp.pad(sent, ((0, 0), (0, slot_rows - cap), (0, lanes - cells)))
    got = lax.all_to_all(sent, "chaos", 0, 0, tiled=True)
    by_slot = got.reshape(n_chaos * slot_rows, lanes)
    my_fields = lax.dynamic_index_in_dim(windows[cap:], my_col_block, axis=2, keepdims=False)
    my_fields = my_fields.reshape(M + 1, cells)
    mean_wide = lax.dynamic_index_in_dim(wide[cap], my_col_block, axis=1, keepdims=False)
    mean_pad = jnp.pad(mean_wide, 1)
    centre = mean_pad[1:-1, 1:-1]
    diagonal = 0.5 * (centre + mean_pad[:-2, 1:-1])
    diagonal = diagonal + 0.5 * (centre + mean_pad[2:, 1:-1])
    diagonal = diagonal + 0.5 * (centre + mean_pad[1:-1, 2:])
    diagonal = diagonal + 0.5 * (centre + mean_pad[1:-1, :-2])
    diagonal = diagonal[trim : trim + patch_rows, trim : trim + patch_cols].reshape(cells)

    blocks, row_of, total = coupling_blocks(M)
    sizes, firsts, padded, offsets = degree_layout(M)
    coeff_of_row = np.full(total, -1, np.int64)
    coeff_of_row[row_of] = np.arange(count)
    row_coeff = jnp.asarray(np.maximum(coeff_of_row, 0), jnp.int32)
    group_ends = jnp.cumsum(lengths).astype(jnp.int32)
    group_starts = (group_ends - lengths).astype(jnp.int32)
    skipped = jnp.sum(
        jnp.where(row_coeff[:, None] >= group_ends[None, :], slot_rows - lengths[None, :], 0), axis=1
    )
    slot_of_row = jnp.where(
        jnp.asarray(coeff_of_row >= 0), row_coeff + skipped, n_chaos * slot_rows - 1
    ).astype(jnp.int32)
    slot_index = jnp.arange(slot_rows, dtype=jnp.int32)
    live = slot_index[None, :] < lengths[:, None]
    coeff = group_starts[:, None] + slot_index[None, :]
    shift = jnp.zeros_like(coeff)
    for d in range(1, 4):
        shift = jnp.where(coeff >= firsts[d], int(offsets[d] - firsts[d]), shift)
    row_of_slot = jnp.where(live, coeff + shift, -1).astype(jnp.int32).reshape(-1)

    row_at = my_row_block * rows - ghost + jnp.arange(patch_rows)
    col_at = my_col_block * width - ghost + jnp.arange(patch_cols)
    inside = ((row_at >= 0) & (row_at < rows * n_space))[:, None] & (
        (col_at >= 0) & (col_at < cols)
    )[None, :]
    inside = inside.reshape(cells)
    local_rows = jnp.arange(patch_rows)
    local_cols = jnp.arange(patch_cols)
    own = ((local_rows >= ghost) & (local_rows < ghost + rows))[:, None] & (
        (local_cols >= ghost) & (local_cols < ghost + width)
    )[None, :]
    own = own.reshape(cells)

    field_rows = -(-(M + 1) // 8) * 8
    field_in = jnp.pad(my_fields, ((0, field_rows - (M + 1)), (0, lanes - cells)))
    masks = jnp.stack([inside.astype(jnp.float32), own.astype(jnp.float32), diagonal])
    masks = jnp.pad(masks, ((0, 5), (0, lanes - cells)))
    mats = [jnp.asarray(blocks[d]) for d in range(4)]
    own_lanes = np.flatnonzero(np.pad(np.ones((rows, width)), ghost).reshape(-1) > 0.5)
    picks = np.zeros((lanes, 128), np.float32)
    picks[own_lanes, np.arange(own_lanes.size)] = 1.0
    state_rows = -(-total // 128) * 128
    solved, partial_rows = pl.pallas_call(
        functools.partial(
            sweeps,
            padded=tuple(int(v) for v in padded),
            offsets=tuple(int(v) for v in offsets),
            cols=patch_cols,
            state_rows=state_rows,
        ),
        out_shape=(
            jax.ShapeDtypeStruct((n_chaos * slot_rows, 128), jnp.float32),
            jax.ShapeDtypeStruct((8, 128), jnp.float32),
        ),
        in_specs=[pl.BlockSpec(memory_space=pltpu.VMEM)] * 10,
        out_specs=(pl.BlockSpec(memory_space=pltpu.VMEM), pl.BlockSpec(memory_space=pltpu.VMEM)),
        scratch_shapes=[pltpu.VMEM((M * padded[d], lanes), jnp.float32) for d in range(4)],
        compiler_params=pltpu.CompilerParams(vmem_limit_bytes=48 * 1024 * 1024),
    )(by_slot, slot_of_row[:, None], row_of_slot[:, None], jnp.asarray(picks), field_in, masks, *mats)
    partials = partial_rows[0, :ITERS]

    own_count = rows * width
    by_slot_out = solved[:, :own_count].reshape(n_chaos, slot_rows, own_count)[:, :cap]
    chunk = cap * rows * width
    payload = jnp.concatenate(
        [
            by_slot_out.reshape(n_chaos, chunk),
            jnp.broadcast_to(partials[None, :], (n_chaos, ITERS)),
        ],
        axis=1,
    )
    back = lax.all_to_all(payload, "chaos", 0, 0, tiled=True)
    out = back[:, :chunk].reshape(n_chaos, cap, rows, width)
    out = jnp.transpose(out, (1, 2, 0, 3)).reshape(cap, rows, cols)
    row_sum = jnp.sum(back[:, chunk:], axis=0)
    spread = jnp.broadcast_to(row_sum[None, :], (n_space, ITERS))
    all_rows = lax.all_to_all(spread, "space", 0, 0, tiled=True)
    norms = jnp.sqrt(jnp.sum(all_rows, axis=0))
    return (out, norms)


def solution(mesh):
    in_specs = (P("chaos", "space", None), P("space", None), P(None, "space", None), P())
    out_specs = (P("chaos", "space", None), P())
    return jax.shard_map(local, mesh=mesh, in_specs=in_specs, out_specs=out_specs, check_vma=False)
```

```python
import functools
import math

import jax
import jax.numpy as jnp
import numpy as np
from jax import lax
from jax.experimental import pallas as pl
from jax.experimental.pallas import tpu as pltpu
from jax.sharding import PartitionSpec as P

M = 12
P_SIZE = 455
ITERS = 3
GHOST = ITERS
MOVED = ITERS + 1


spectrum_low = 0.05
spectrum_high = 3.0


def index_key(entry):
    return tuple((int(value) for value in entry))


def chaos_tables(terms):
    indices = [np.zeros(terms, dtype=np.int64)]
    for first in range(terms):
        entry = np.zeros(terms, dtype=np.int64)
        entry[first] += 1
        indices.append(entry)
    for first in range(terms):
        for second in range(first, terms):
            entry = np.zeros(terms, dtype=np.int64)
            entry[first] += 1
            entry[second] += 1
            indices.append(entry)
    for first in range(terms):
        for second in range(first, terms):
            for third in range(second, terms):
                entry = np.zeros(terms, dtype=np.int64)
                entry[first] += 1
                entry[second] += 1
                entry[third] += 1
                indices.append(entry)
    lookup = {}
    for number, entry in enumerate(indices):
        lookup[index_key(entry)] = number
    count = len(indices)
    upward = np.full((count, terms), count, dtype=np.int64)
    downward = np.full((count, terms), count, dtype=np.int64)
    up_coef = np.zeros((count, terms))
    down_coef = np.zeros((count, terms))
    for number, entry in enumerate(indices):
        for term in range(terms):
            if entry.sum() < 3:
                other = entry.copy()
                other[term] += 1
                upward[number, term] = lookup[index_key(other)]
                up_coef[number, term] = math.sqrt(entry[term] + 1)
            if entry[term] > 0:
                other = entry.copy()
                other[term] -= 1
                downward[number, term] = lookup[index_key(other)]
                down_coef[number, term] = math.sqrt(entry[term])
    return (
        upward.astype(np.int32),
        downward.astype(np.int32),
        up_coef.astype(np.float32),
        down_coef.astype(np.float32),
    )


def degree_layout(terms):
    sizes = [1, terms, terms * (terms + 1) // 2, terms * (terms + 1) * (terms + 2) // 6]
    firsts = np.cumsum([0] + sizes[:-1])
    padded = [-(-size // 8) * 8 for size in sizes]
    offsets = np.cumsum([0] + padded[:-1])
    return sizes, firsts, padded, offsets


def coupling_blocks(terms):
    upward, downward, up_coef, down_coef = chaos_tables(terms)
    sizes, firsts, padded, offsets = degree_layout(terms)
    count = sum(sizes)
    total = sum(padded)
    row_of = np.zeros(count, np.int64)
    for d in range(4):
        row_of[firsts[d] : firsts[d] + sizes[d]] = offsets[d] + np.arange(sizes[d])
    dense = np.zeros((terms, total, total), np.float64)
    for p in range(count):
        for k in range(terms):
            if upward[p, k] < count:
                dense[k, row_of[p], row_of[upward[p, k]]] = up_coef[p, k]
            if downward[p, k] < count:
                dense[k, row_of[p], row_of[downward[p, k]]] = down_coef[p, k]

    def block(out_degrees, in_degree):
        rows = np.concatenate([offsets[d] + np.arange(padded[d]) for d in out_degrees])
        cols = offsets[in_degree] + np.arange(padded[in_degree])
        part = dense[:, rows][:, :, cols]
        return np.transpose(part, (1, 0, 2)).reshape(len(rows), terms * len(cols)).astype(np.float32)

    return {
        0: block((1,), 0),
        1: block((0, 2), 1),
        2: block((1, 3), 2),
        3: block((2,), 3),
    }, row_of, total


def neighbour(values, step):
    blank = jnp.zeros(values.shape[:-1] + (abs(step),), values.dtype)
    if step > 0:
        return jnp.concatenate([values[..., step:], blank], axis=-1)
    return jnp.concatenate([blank, values[..., :step]], axis=-1)


def exact_dot(left, right):
    return jnp.dot(left, right, precision=lax.Precision.HIGHEST, preferred_element_type=jnp.float32)


def pick_dot(left, right, split_left):
    ones, values = (right, left) if split_left else (left, right)
    ones = ones.astype(jnp.bfloat16)
    high = values.astype(jnp.bfloat16)
    rest = values - high.astype(jnp.float32)
    middle = rest.astype(jnp.bfloat16)
    low = (rest - middle.astype(jnp.float32)).astype(jnp.bfloat16)
    total = None
    for part in (high, middle, low):
        pair = (part, ones) if split_left else (ones, part)
        step = jnp.dot(*pair, preferred_element_type=jnp.float32)
        total = step if total is None else total + step
    return total


def sweeps(slots_ref, slot_of_row_ref, row_of_slot_ref, picks_ref, field_ref, mask_ref,
           w0_ref, w1_ref, w2_ref, w3_ref, out_ref, part_ref,
           s0_ref, s1_ref, s2_ref, s3_ref, *, padded, offsets, cols, state_rows):
    lanes = slots_ref.shape[1]
    total = slot_of_row_ref.shape[0]
    n_slots = slots_ref.shape[0]
    take = lax.broadcasted_iota(jnp.int32, (total, n_slots), 1) == slot_of_row_ref[...]
    rhs = pick_dot(take.astype(jnp.float32), slots_ref[...], False)
    shifts = (cols, lanes - cols, lanes - 1, 1)

    def near(values, shift):
        return pltpu.roll(values, shift, 1)

    fields = field_ref[...]
    inside = mask_ref[0:1, :] > 0.5
    own = mask_ref[1:2, :] > 0.5
    weights = [[0.5 * (fields[k : k + 1] + near(fields, s)[k : k + 1]) for s in shifts] for k in range(M + 1)]
    diagonal = jnp.where(inside, mask_ref[2:3, :], 1.0)
    stacks = (s0_ref, s1_ref, s2_ref, s3_ref)
    mats = (w0_ref, w1_ref, w2_ref, w3_ref)

    def operator(tiles):
        diffs = [tiles - near(tiles, s) for s in shifts]
        base = None
        for k in range(M + 1):
            term = weights[k][0] * diffs[0]
            for n in range(1, 4):
                term = term + weights[k][n] * diffs[n]
            if k == 0:
                base = term
                continue
            for d in range(4):
                stacks[d][(k - 1) * padded[d] : k * padded[d], :] = term[offsets[d] : offsets[d] + padded[d]]
        mixed = [
            jnp.dot(
                mats[d][...],
                stacks[d][...],
                precision=lax.Precision.HIGH,
                preferred_element_type=jnp.float32,
            )
            for d in range(4)
        ]
        p0, p1 = padded[0], padded[1]
        coupled = jnp.concatenate(
            [mixed[1][:p0], mixed[2][:p1] + mixed[0], mixed[3] + mixed[1][p0:], mixed[2][p1:]], axis=0
        )
        return base + coupled

    theta = (spectrum_high + spectrum_low) / 2.0
    delta = (spectrum_high - spectrum_low) / 2.0
    sigma = theta / delta
    rho = 1.0 / sigma
    residual = rhs
    solution = jnp.zeros_like(residual)
    direction = jnp.where(inside, residual / diagonal / theta, 0.0)
    lane = lax.broadcasted_iota(jnp.int32, (8, 128), 1)
    partial_out = jnp.zeros((8, 128), jnp.float32)
    for sweep_index in range(ITERS):
        solution = solution + direction
        residual = residual - operator(direction)
        value = jnp.sum(jnp.where(own, residual * residual, 0.0))
        partial_out = jnp.where(lane == sweep_index, value, partial_out)
        if sweep_index + 1 < ITERS:
            rho_new = 1.0 / (2.0 * sigma - rho)
            direction = rho_new * rho * direction + 2.0 * rho_new / delta * (residual / diagonal)
            direction = jnp.where(inside, direction, 0.0)
            rho = rho_new
    own_cells = pick_dot(solution, picks_ref[...], True)
    own_cells = jnp.concatenate(
        [own_cells, jnp.zeros((state_rows - total, own_cells.shape[1]), jnp.float32)], axis=0
    )
    put = lax.broadcasted_iota(jnp.int32, (n_slots, state_rows), 1) == row_of_slot_ref[...]
    out_ref[...] = pick_dot(put.astype(jnp.float32), own_cells, False)
    part_ref[...] = partial_out


def local(forcing, mean_field, modes, lengths):
    cap, rows, cols = forcing.shape
    n_space = lax.axis_size("space")
    n_chaos = lax.axis_size("chaos")
    my_row_block = lax.axis_index("space")
    my_col_block = lax.axis_index("chaos")
    width = cols // n_chaos
    ghost, moved = GHOST, MOVED
    assert rows >= moved and moved % width == 0 and width * n_chaos == cols
    patch_rows, patch_cols = rows + 2 * ghost, width + 2 * ghost
    cells = patch_rows * patch_cols
    count = P_SIZE

    fields = jnp.concatenate([mean_field[None], mean_field[None] * modes], axis=0)
    block = jnp.concatenate([forcing, fields], axis=0)
    down_pairs = [(i, i + 1) for i in range(n_space - 1)]
    up_pairs = [(i + 1, i) for i in range(n_space - 1)]
    above = lax.ppermute(block[:, rows - moved :], "space", down_pairs)
    below = lax.ppermute(block[:, :moved], "space", up_pairs)
    tall = jnp.concatenate([above, block, below], axis=1)
    tall = jnp.pad(tall, ((0, 0), (0, 0), (moved, moved)))

    side = moved // width
    wide_rows = rows + 2 * moved
    pieces = tall.reshape(tall.shape[0], wide_rows, n_chaos + 2 * side, width)
    wide = jnp.concatenate(
        [pieces[:, :, j : j + n_chaos] for j in range(2 * side + 1)], axis=-1
    )
    trim = moved - ghost
    windows = wide[:, trim : wide_rows - trim, :, trim : width + 2 * moved - trim]
    lanes = -(-cells // 128) * 128
    assert cells + patch_cols <= lanes
    slot_rows = -(-(cap + 1) // 8) * 8
    sent = jnp.transpose(windows[:cap], (2, 0, 1, 3)).reshape(n_chaos, cap, cells)
    sent = jnp.pad(sent, ((0, 0), (0, slot_rows - cap), (0, lanes - cells)))
    got = lax.all_to_all(sent, "chaos", 0, 0, tiled=True)
    by_slot = got.reshape(n_chaos * slot_rows, lanes)
    my_fields = lax.dynamic_index_in_dim(windows[cap:], my_col_block, axis=2, keepdims=False)
    my_fields = my_fields.reshape(M + 1, cells)
    mean_wide = lax.dynamic_index_in_dim(wide[cap], my_col_block, axis=1, keepdims=False)
    mean_pad = jnp.pad(mean_wide, 1)
    centre = mean_pad[1:-1, 1:-1]
    diagonal = 0.5 * (centre + mean_pad[:-2, 1:-1])
    diagonal = diagonal + 0.5 * (centre + mean_pad[2:, 1:-1])
    diagonal = diagonal + 0.5 * (centre + mean_pad[1:-1, 2:])
    diagonal = diagonal + 0.5 * (centre + mean_pad[1:-1, :-2])
    diagonal = diagonal[trim : trim + patch_rows, trim : trim + patch_cols].reshape(cells)

    blocks, row_of, total = coupling_blocks(M)
    sizes, firsts, padded, offsets = degree_layout(M)
    coeff_of_row = np.full(total, -1, np.int64)
    coeff_of_row[row_of] = np.arange(count)
    row_coeff = jnp.asarray(np.maximum(coeff_of_row, 0), jnp.int32)
    group_ends = jnp.cumsum(lengths).astype(jnp.int32)
    group_starts = (group_ends - lengths).astype(jnp.int32)
    skipped = jnp.sum(
        jnp.where(row_coeff[:, None] >= group_ends[None, :], slot_rows - lengths[None, :], 0), axis=1
    )
    slot_of_row = jnp.where(
        jnp.asarray(coeff_of_row >= 0), row_coeff + skipped, n_chaos * slot_rows - 1
    ).astype(jnp.int32)
    slot_index = jnp.arange(slot_rows, dtype=jnp.int32)
    live = slot_index[None, :] < lengths[:, None]
    coeff = group_starts[:, None] + slot_index[None, :]
    shift = jnp.zeros_like(coeff)
    for d in range(1, 4):
        shift = jnp.where(coeff >= firsts[d], int(offsets[d] - firsts[d]), shift)
    row_of_slot = jnp.where(live, coeff + shift, -1).astype(jnp.int32).reshape(-1)

    row_at = my_row_block * rows - ghost + jnp.arange(patch_rows)
    col_at = my_col_block * width - ghost + jnp.arange(patch_cols)
    inside = ((row_at >= 0) & (row_at < rows * n_space))[:, None] & (
        (col_at >= 0) & (col_at < cols)
    )[None, :]
    inside = inside.reshape(cells)
    local_rows = jnp.arange(patch_rows)
    local_cols = jnp.arange(patch_cols)
    own = ((local_rows >= ghost) & (local_rows < ghost + rows))[:, None] & (
        (local_cols >= ghost) & (local_cols < ghost + width)
    )[None, :]
    own = own.reshape(cells)

    field_rows = -(-(M + 1) // 8) * 8
    field_in = jnp.pad(my_fields, ((0, field_rows - (M + 1)), (0, lanes - cells)))
    masks = jnp.stack([inside.astype(jnp.float32), own.astype(jnp.float32), diagonal])
    masks = jnp.pad(masks, ((0, 5), (0, lanes - cells)))
    mats = [jnp.asarray(blocks[d]) for d in range(4)]
    own_lanes = np.flatnonzero(np.pad(np.ones((rows, width)), ghost).reshape(-1) > 0.5)
    picks = np.zeros((lanes, 128), np.float32)
    picks[own_lanes, np.arange(own_lanes.size)] = 1.0
    state_rows = -(-total // 128) * 128
    solved, partial_rows = pl.pallas_call(
        functools.partial(
            sweeps,
            padded=tuple(int(v) for v in padded),
            offsets=tuple(int(v) for v in offsets),
            cols=patch_cols,
            state_rows=state_rows,
        ),
        out_shape=(
            jax.ShapeDtypeStruct((n_chaos * slot_rows, 128), jnp.float32),
            jax.ShapeDtypeStruct((8, 128), jnp.float32),
        ),
        in_specs=[pl.BlockSpec(memory_space=pltpu.VMEM)] * 10,
        out_specs=(pl.BlockSpec(memory_space=pltpu.VMEM), pl.BlockSpec(memory_space=pltpu.VMEM)),
        scratch_shapes=[pltpu.VMEM((M * padded[d], lanes), jnp.float32) for d in range(4)],
        compiler_params=pltpu.CompilerParams(vmem_limit_bytes=48 * 1024 * 1024),
    )(by_slot, slot_of_row[:, None], row_of_slot[:, None], jnp.asarray(picks), field_in, masks, *mats)
    partials = partial_rows[0, :ITERS]

    own_count = rows * width
    by_slot_out = solved[:, :own_count].reshape(n_chaos, slot_rows, own_count)[:, :cap]
    chunk = cap * rows * width
    payload = jnp.concatenate(
        [
            by_slot_out.reshape(n_chaos, chunk),
            jnp.broadcast_to(partials[None, :], (n_chaos, ITERS)),
            jnp.zeros((n_chaos, -(-(chunk + ITERS) // 128) * 128 - chunk - ITERS), jnp.float32),
        ],
        axis=1,
    )
    back = lax.all_to_all(payload, "chaos", 0, 0, tiled=True)
    out = back[:, :chunk].reshape(n_chaos, cap, rows, width)
    out = jnp.transpose(out, (1, 2, 0, 3)).reshape(cap, rows, cols)
    row_sum = jnp.sum(back[:, chunk : chunk + ITERS], axis=0)
    spread = jnp.broadcast_to(row_sum[None, :], (n_space, ITERS))
    all_rows = lax.all_to_all(spread, "space", 0, 0, tiled=True)
    norms = jnp.sqrt(jnp.sum(all_rows, axis=0))
    return (out, norms)


def solution(mesh):
    in_specs = (P("chaos", "space", None), P("space", None), P(None, "space", None), P())
    out_specs = (P("chaos", "space", None), P())
    return jax.shard_map(local, mesh=mesh, in_specs=in_specs, out_specs=out_specs, check_vma=False)
```
